128 devices in a mesh: ctx: 8 (over y_hi, z), chan: 16 (over y_lo, x, core).
Axes of the slice: x: 4, y: 4 (y_hi: 2, y_lo: 2; y = y_hi * 2 + y_lo), z: 4, core: 2. Of those that a mesh axis runs over, the one named last changes fastest.
Arguments:
- tokens: bfloat16 [16384, 4096], P(('ctx', 'chan')), may hold values from -6 to 6
- in_weight: bfloat16 [3, 4096, 4096], P(None, None, 'chan'), may hold values from -0.09375 to 0.09375
- short_weight: float32 [3, 3, 4096], P(None, None, 'chan'), may hold values from -3 to 3
- decay_rate: float32 [16, 4096], P(None, 'chan'), may hold values from 1.2207031e-05 to 0.0333333333
- residue: float32 [16, 4096], P(None, 'chan'), may hold values from -1.5 to 1.5
- skip_gain: float32 [4096], P('chan'), may hold values from -4 to 4
- out_weight: bfloat16 [4096, 4096], P('chan'), may hold values from -0.09375 to 0.09375
Outputs:
- block_out: bfloat16 [16384, 4096], P(('ctx', 'chan'))
The draws below stay inside these ranges and needn't reach their ends.
All inputs are finite; a program needn't handle non-finite values.
Results may differ from the reference program's by a relative error of at most 0.02.
Values may be sent and summed in bfloat16 or wider, within the bound.
No kernel may reach another device: no remote copies, remote signals or barrier semaphores. Data moves between devices by JAX's collectives and lax.ppermute only.
A program may use at most 128 MiB of HBM per device.

```python
import math
import jax
import jax.numpy as jnp
from jax import lax

D = 4096
MODES = 16
TAPS = 3
GROUP = 256
SEQ = 16384


def draw_decay_rate(key, part):
    slow_key = jax.random.fold_in(key, 11)
    low_key = jax.random.fold_in(key, 12)
    high_key = jax.random.fold_in(key, 13)
    share = 0.5
    slow_mask = jax.random.uniform(slow_key, (MODES, D), jnp.float32) < share
    slow_log = jax.random.uniform(low_key, (MODES, D), jnp.float32, math.log(0.2 / SEQ), math.log(2.0 / SEQ))
    fast_log = jax.random.uniform(high_key, (MODES, D), jnp.float32, math.log(1.0 / 50.0), math.log(1.0 / 30.0))
    return jnp.exp(jnp.where(slow_mask, slow_log, fast_log)).astype(jnp.float32)


def steps_of(stream_key, extent, cuts, least, high):
    factor_of = 1.0
    for axis_at, blocks in cuts:
        heights = jax.random.uniform(jax.random.fold_in(jax.random.fold_in(stream_key, 6), axis_at), (blocks,), jnp.float32, least / len(cuts), high / len(cuts))
        factor_of = factor_of * jnp.repeat(jnp.exp(heights), extent[axis_at] // blocks).reshape((-1,) + (1,) * (len(extent) - 1 - axis_at))
    return factor_of


def noise(stream_key, dims, spread, reach, pieces=(), kind=jnp.bfloat16):
    values = jax.random.normal(stream_key, dims, jnp.float32) * spread
    if len(pieces) > 0:
        values = steps_of(stream_key, dims, pieces, -0.22, 0.18) * values
    return jnp.clip(values, min=-reach, max=reach).astype(kind)


def setup_inputs(seed: int = 0) -> dict:
    seeds = jax.random.split(jax.random.key(seed), 8)
    return {
        "tokens": noise(seeds[0], (SEQ, D), 1.0, 6.0, ((0, 128),)),
        "in_weight": noise(seeds[1], (3, D, D), D ** -0.5, 0.09375, ((2, 16),)),
        "short_weight": noise(seeds[2], (TAPS, 3, D), 0.6, 3.0, ((2, 16),), jnp.float32),
        "decay_rate": draw_decay_rate(jax.random.fold_in(seeds[7], 71), 0),
        "residue": noise(seeds[4], (MODES, D), 0.25, 1.5, ((1, 16),), jnp.float32),
        "skip_gain": noise(seeds[5], (D,), 1.0, 4.0, ((0, 16),), jnp.float32),
        "out_weight": noise(seeds[6], (D, D), D ** -0.5, 0.09375, ((0, 16),)),
    }


def reference(tokens, in_weight, short_weight, decay_rate, residue, skip_gain, out_weight):
    projected = jnp.stack([jnp.dot(tokens, in_weight[kind], preferred_element_type=jnp.float32) for kind in range(3)], 1).astype(jnp.bfloat16)
    padded = jnp.concatenate([jnp.zeros((TAPS - 1, 3, D), jnp.bfloat16), projected], 0)
    features = jnp.zeros((SEQ, 3, D), jnp.float32)
    for offset in range(TAPS):
        features = features + short_weight[offset] * padded[TAPS - 1 - offset:TAPS - 1 - offset + SEQ].astype(jnp.float32)
    query_part = features[:, 0]
    driven = features[:, 1] * features[:, 2]
    poles = jnp.exp(-decay_rate)
    mode_gain = residue * jnp.sqrt(2.0 * decay_rate)

    def advance(carried_state, token_drive):
        carried_state = poles * carried_state + token_drive[None, :]
        return (carried_state, lax.optimization_barrier(jnp.sum(mode_gain * carried_state, 0)))
    _, long_conv = lax.scan(advance, jnp.zeros((MODES, D), jnp.float32), driven)
    gated = (query_part * (long_conv + skip_gain * driven)).astype(jnp.bfloat16)

    def add_group(running, group_idx):
        columns = lax.dynamic_slice_in_dim(gated, group_idx * GROUP, GROUP, 1)
        weight_rows = lax.dynamic_slice_in_dim(out_weight, group_idx * GROUP, GROUP, 0)
        group_part = jnp.dot(columns, weight_rows, preferred_element_type=jnp.float32).astype(jnp.bfloat16)
        group_part = lax.optimization_barrier(group_part)
        return (running + group_part.astype(jnp.float32), None)
    summed, _ = lax.scan(add_group, jnp.zeros((SEQ, D), jnp.float32), jnp.arange(D // GROUP, dtype=jnp.int32))
    return summed.astype(jnp.bfloat16)
```

```python
import functools

import jax
import jax.numpy as jnp
from jax import lax
from jax.experimental import pallas as pl
from jax.sharding import Mesh
from jax.sharding import PartitionSpec as P

SEGS = 8
LANES = 128


def from_behind(array, axis, by):
    size = lax.axis_size(axis)
    pairs = [(i, i + by) for i in range(size) if 0 <= i + by < size]
    return lax.ppermute(array, axis, pairs)


def scan_kernel(x_ref, p_ref, g_ref, s0_ref, *out_refs, steps, with_y):
    modes = p_ref.shape[0]
    poles = [p_ref[r] for r in range(modes)]
    gains = [g_ref[r] for r in range(modes)]
    if with_y:
        y_ref, end_ref = out_refs
    else:
        (end_ref,) = out_refs

    def body(k, state):
        drive = x_ref[k]
        state = tuple(poles[r] * state[r] + drive for r in range(modes))
        if with_y:
            acc = gains[0] * state[0]
            for r in range(1, modes):
                acc = acc + gains[r] * state[r]
            y_ref[k] = acc
        return state

    state = lax.fori_loop(0, steps, body, tuple(s0_ref[r] for r in range(modes)), unroll=2)
    for r in range(modes):
        end_ref[r] = state[r]


def modal_scan(x_t, poles_b, gains_b, init, with_y):
    steps, segs, chans = x_t.shape
    modes = poles_b.shape[0]
    state_spec = pl.BlockSpec((modes, segs, LANES), lambda i: (0, 0, i))
    x_spec = pl.BlockSpec((steps, segs, LANES), lambda i: (0, 0, i))
    end_shape = jax.ShapeDtypeStruct((modes, segs, chans), jnp.float32)
    if with_y:
        out_shape = (jax.ShapeDtypeStruct((steps, segs, chans), jnp.float32), end_shape)
        out_specs = (x_spec, state_spec)
    else:
        out_shape = (end_shape,)
        out_specs = (state_spec,)
    return pl.pallas_call(
        functools.partial(scan_kernel, steps=steps, with_y=with_y),
        grid=(chans // LANES,),
        in_specs=[x_spec, state_spec, state_spec, state_spec],
        out_specs=out_specs,
        out_shape=out_shape,
    )(x_t, poles_b, gains_b, init)


def local(tokens, in_weight, short_weight, decay_rate, residue, skip_gain, out_weight):
    group_chans = in_weight.shape[2]
    filter_taps = short_weight.shape[0]
    modes = decay_rate.shape[0]
    by_chip = lax.all_gather(tokens, "chip", axis=0)
    by_core = lax.all_gather(by_chip, "core", axis=0)
    cores, chips, rows = by_core.shape[:3]
    projected = jnp.einsum(
        "abld,jdc->abljc", by_core, in_weight, preferred_element_type=jnp.float32
    ).astype(jnp.bfloat16)
    seq_rows = cores * chips * rows
    projected = projected.transpose(1, 0, 2, 3, 4).reshape(seq_rows, 3, group_chans)
    earlier_rows = from_behind(projected[seq_rows - (filter_taps - 1) :], "ctx", 1)
    padded = jnp.concatenate([earlier_rows, projected], 0)
    features = jnp.zeros((seq_rows, 3, group_chans), jnp.float32)
    for offset in range(filter_taps):
        features = features + short_weight[offset] * padded[
            filter_taps - 1 - offset : filter_taps - 1 - offset + seq_rows
        ].astype(jnp.float32)
    query_part = features[:, 0]
    driven = features[:, 1] * features[:, 2]

    seg_len = seq_rows // SEGS
    poles = jnp.exp(-decay_rate)
    mode_gain = residue * jnp.sqrt(2.0 * decay_rate)
    poles_b = jnp.broadcast_to(poles[:, None, :], (modes, SEGS, group_chans))
    gains_b = jnp.broadcast_to(mode_gain[:, None, :], (modes, SEGS, group_chans))
    x_t = driven.reshape(SEGS, seg_len, group_chans).transpose(1, 0, 2)
    zero_init = jnp.zeros((modes, SEGS, group_chans), jnp.float32)
    (seg_end,) = modal_scan(x_t, poles_b, gains_b, zero_init, False)

    seg_pos = jnp.arange(SEGS, dtype=jnp.float32)
    tail_weight = jnp.exp(-decay_rate[:, None, :] * seg_len * (SEGS - 1.0 - seg_pos)[None, :, None])
    own_state = jnp.sum(tail_weight * seg_end, 1)
    states = lax.all_gather(own_state, "ctx", axis=0)
    blocks = states.shape[0]
    mine = lax.axis_index("ctx").astype(jnp.float32)
    block_pos = jnp.arange(blocks, dtype=jnp.float32)
    block_gap = mine - 1.0 - block_pos
    block_weight = jnp.where(
        (block_gap >= 0.0)[:, None, None],
        jnp.exp(-decay_rate[None] * seq_rows * jnp.maximum(block_gap, 0.0)[:, None, None]),
        0.0,
    )
    entering = jnp.sum(block_weight * states, 0)
    seg_gap = seg_pos[:, None] - 1.0 - seg_pos[None, :]
    seg_mix = jnp.where(
        (seg_gap >= 0.0)[:, :, None, None],
        jnp.exp(-decay_rate[None, None] * seg_len * jnp.maximum(seg_gap, 0.0)[:, :, None, None]),
        0.0,
    )
    seg_init = jnp.einsum("jirc,ric->rjc", seg_mix, seg_end, precision=lax.Precision.HIGHEST)
    seg_init = seg_init + jnp.exp(
        -decay_rate[:, None, :] * seg_len * seg_pos[None, :, None]
    ) * entering[:, None, :]
    long_t, _ = modal_scan(x_t, poles_b, gains_b, seg_init, True)
    long_conv = long_t.transpose(1, 0, 2).reshape(seq_rows, group_chans)

    gated = (query_part * (long_conv + skip_gain * driven)).astype(jnp.bfloat16)
    gated = gated.reshape(chips, cores, rows, group_chans).transpose(1, 0, 2, 3)
    rounded = jnp.einsum(
        "ablc,cn->abln", gated, out_weight, preferred_element_type=jnp.float32
    ).astype(jnp.bfloat16)
    over_core = lax.psum_scatter(rounded, "core", scatter_dimension=0, tiled=False)
    return lax.psum_scatter(over_core, "chip", scatter_dimension=0, tiled=False)


def solution(mesh):
    shape = mesh.devices.shape
    split = Mesh(mesh.devices.reshape(shape[0], shape[1] // 2, 2), ("ctx", "chip", "core"))
    chan = ("chip", "core")
    return jax.shard_map(
        local,
        mesh=split,
        in_specs=(
            P(("ctx",) + chan, None),
            P(None, None, chan),
            P(None, None, chan),
            P(None, chan),
            P(None, chan),
            P(chan),
            P(chan, None),
        ),
        out_specs=P(("ctx",) + chan, None),
        check_vma=False,
    )
```

```python
import functools

import jax
import jax.numpy as jnp
from jax import lax
from jax.experimental import pallas as pl
from jax.sharding import PartitionSpec as P

SEGS = 8
LANES = 128
CHUNKS = 2


def from_behind(array, axis, by):
    size = lax.axis_size(axis)
    pairs = [(i, i + by) for i in range(size) if 0 <= i + by < size]
    return lax.ppermute(array, axis, pairs)


def scan_kernel(x_ref, p_ref, g_ref, s0_ref, *out_refs, steps, with_y):
    modes = p_ref.shape[0]
    poles = [p_ref[r] for r in range(modes)]
    gains = [g_ref[r] for r in range(modes)]
    if with_y:
        y_ref, end_ref = out_refs
    else:
        (end_ref,) = out_refs

    def body(k, state):
        drive = x_ref[k]
        state = tuple(poles[r] * state[r] + drive for r in range(modes))
        if with_y:
            acc = gains[0] * state[0]
            for r in range(1, modes):
                acc = acc + gains[r] * state[r]
            y_ref[k] = acc
        return state

    state = lax.fori_loop(0, steps, body, tuple(s0_ref[r] for r in range(modes)), unroll=2)
    for r in range(modes):
        end_ref[r] = state[r]


def modal_scan(x_t, poles_b, gains_b, init, with_y):
    steps, segs, chans = x_t.shape
    modes = poles_b.shape[0]
    state_spec = pl.BlockSpec((modes, segs, LANES), lambda i: (0, 0, i))
    x_spec = pl.BlockSpec((steps, segs, LANES), lambda i: (0, 0, i))
    end_shape = jax.ShapeDtypeStruct((modes, segs, chans), jnp.float32)
    if with_y:
        out_shape = (jax.ShapeDtypeStruct((steps, segs, chans), jnp.float32), end_shape)
        out_specs = (x_spec, state_spec)
    else:
        out_shape = (end_shape,)
        out_specs = (state_spec,)
    return pl.pallas_call(
        functools.partial(scan_kernel, steps=steps, with_y=with_y),
        grid=(chans // LANES,),
        in_specs=[x_spec, state_spec, state_spec, state_spec],
        out_specs=out_specs,
        out_shape=out_shape,
    )(x_t, poles_b, gains_b, init)


def local(tokens, in_weight, short_weight, decay_rate, residue, skip_gain, out_weight):
    group_chans = in_weight.shape[2]
    filter_taps = short_weight.shape[0]
    modes = decay_rate.shape[0]
    chunks = CHUNKS
    rows = tokens.shape[0] // chunks
    parts = []
    for q in range(chunks):
        gathered = lax.all_gather(tokens[q * rows : (q + 1) * rows], "chan", axis=0)
        parts.append(
            jnp.einsum("sld,jdc->sljc", gathered, in_weight, preferred_element_type=jnp.float32).astype(
                jnp.bfloat16
            )
        )
    sources = parts[0].shape[0]
    seq_rows = sources * chunks * rows
    projected = jnp.stack(parts, 1).reshape(seq_rows, 3, group_chans)
    earlier_rows = from_behind(projected[seq_rows - (filter_taps - 1) :], "ctx", 1)
    padded = jnp.concatenate([earlier_rows, projected], 0)
    features = jnp.zeros((seq_rows, 3, group_chans), jnp.float32)
    for offset in range(filter_taps):
        features = features + short_weight[offset] * padded[
            filter_taps - 1 - offset : filter_taps - 1 - offset + seq_rows
        ].astype(jnp.float32)
    query_part = features[:, 0]
    driven = features[:, 1] * features[:, 2]

    seg_len = seq_rows // SEGS
    poles = jnp.exp(-decay_rate)
    mode_gain = residue * jnp.sqrt(2.0 * decay_rate)
    poles_b = jnp.broadcast_to(poles[:, None, :], (modes, SEGS, group_chans))
    gains_b = jnp.broadcast_to(mode_gain[:, None, :], (modes, SEGS, group_chans))
    x_t = driven.reshape(SEGS, seg_len, group_chans).transpose(1, 0, 2)
    zero_init = jnp.zeros((modes, SEGS, group_chans), jnp.float32)
    (seg_end,) = modal_scan(x_t, poles_b, gains_b, zero_init, False)

    seg_pos = jnp.arange(SEGS, dtype=jnp.float32)
    tail_weight = jnp.exp(-decay_rate[:, None, :] * seg_len * (SEGS - 1.0 - seg_pos)[None, :, None])
    own_state = jnp.sum(tail_weight * seg_end, 1)
    blocks = lax.axis_size("ctx")
    mine = lax.axis_index("ctx")
    prefix = own_state
    reach = 1
    while reach < blocks:
        shifted = from_behind(prefix, "ctx", reach)
        prefix = prefix + jnp.where(mine >= reach, jnp.exp(-decay_rate * (seq_rows * reach)), 0.0) * shifted
        reach *= 2
    entering = jnp.where(mine >= 1, from_behind(prefix, "ctx", 1), 0.0)
    seg_gap = seg_pos[:, None] - 1.0 - seg_pos[None, :]
    seg_mix = jnp.where(
        (seg_gap >= 0.0)[:, :, None, None],
        jnp.exp(-decay_rate[None, None] * seg_len * jnp.maximum(seg_gap, 0.0)[:, :, None, None]),
        0.0,
    )
    seg_init = jnp.einsum("jirc,ric->rjc", seg_mix, seg_end, precision=lax.Precision.HIGHEST)
    seg_init = seg_init + jnp.exp(
        -decay_rate[:, None, :] * seg_len * seg_pos[None, :, None]
    ) * entering[:, None, :]
    long_t, _ = modal_scan(x_t, poles_b, gains_b, seg_init, True)
    long_conv = long_t.transpose(1, 0, 2).reshape(seq_rows, group_chans)

    gated = (query_part * (long_conv + skip_gain * driven)).astype(jnp.bfloat16)
    gated = gated.reshape(sources, chunks, rows, group_chans)
    outs = []
    for q in range(chunks):
        rounded = jnp.einsum(
            "slc,cn->sln", gated[:, q], out_weight, preferred_element_type=jnp.float32
        ).astype(jnp.bfloat16)
        outs.append(lax.psum_scatter(rounded, "chan", scatter_dimension=0, tiled=False))
    return jnp.concatenate(outs, 0)


def solution(mesh):
    return jax.shard_map(
        local,
        mesh=mesh,
        in_specs=(
            P(("ctx", "chan"), None),
            P(None, None, "chan"),
            P(None, None, "chan"),
            P(None, "chan"),
            P(None, "chan"),
            P("chan"),
            P("chan", None),
        ),
        out_specs=P(("ctx", "chan"), None),
        check_vma=False,
    )
```

```python
import functools

import jax
import jax.numpy as jnp
from jax import lax
from jax.experimental import pallas as pl
from jax.sharding import PartitionSpec as P

SEGS = 8
LANES = 128
CHUNKS = 1


def from_behind(array, axis, by):
    size = lax.axis_size(axis)
    pairs = [(i, i + by) for i in range(size) if 0 <= i + by < size]
    return lax.ppermute(array, axis, pairs)


def scan_kernel(x_ref, p_ref, g_ref, s0_ref, *out_refs, steps, with_y):
    modes = p_ref.shape[0]
    poles = [p_ref[r] for r in range(modes)]
    gains = [g_ref[r] for r in range(modes)]
    if with_y:
        y_ref, end_ref = out_refs
    else:
        (end_ref,) = out_refs

    def body(k, state):
        drive = x_ref[k]
        state = tuple(poles[r] * state[r] + drive for r in range(modes))
        if with_y:
            acc = gains[0] * state[0]
            for r in range(1, modes):
                acc = acc + gains[r] * state[r]
            y_ref[k] = acc
        return state

    state = lax.fori_loop(0, steps, body, tuple(s0_ref[r] for r in range(modes)), unroll=2)
    for r in range(modes):
        end_ref[r] = state[r]


def modal_scan(x_t, poles_b, gains_b, init, with_y):
    steps, segs, chans = x_t.shape
    modes = poles_b.shape[0]
    state_spec = pl.BlockSpec((modes, segs, LANES), lambda i: (0, 0, i))
    x_spec = pl.BlockSpec((steps, segs, LANES), lambda i: (0, 0, i))
    end_shape = jax.ShapeDtypeStruct((modes, segs, chans), jnp.float32)
    if with_y:
        out_shape = (jax.ShapeDtypeStruct((steps, segs, chans), jnp.float32), end_shape)
        out_specs = (x_spec, state_spec)
    else:
        out_shape = (end_shape,)
        out_specs = (state_spec,)
    return pl.pallas_call(
        functools.partial(scan_kernel, steps=steps, with_y=with_y),
        grid=(chans // LANES,),
        in_specs=[x_spec, state_spec, state_spec, state_spec],
        out_specs=out_specs,
        out_shape=out_shape,
    )(x_t, poles_b, gains_b, init)


def local(tokens, in_weight, short_weight, decay_rate, residue, skip_gain, out_weight):
    group_chans = in_weight.shape[2]
    filter_taps = short_weight.shape[0]
    modes = decay_rate.shape[0]
    chunks = CHUNKS
    rows = tokens.shape[0] // chunks
    parts = []
    for q in range(chunks):
        gathered = lax.all_gather(tokens[q * rows : (q + 1) * rows], "chan", axis=0)
        parts.append(
            jnp.einsum("sld,jdc->sljc", gathered, in_weight, preferred_element_type=jnp.float32).astype(
                jnp.bfloat16
            )
        )
    sources = parts[0].shape[0]
    seq_rows = sources * chunks * rows
    projected = jnp.stack(parts, 1).reshape(seq_rows, 3, group_chans)
    earlier_rows = from_behind(projected[seq_rows - (filter_taps - 1) :], "ctx", 1)
    padded = jnp.concatenate([earlier_rows, projected], 0)
    features = jnp.zeros((seq_rows, 3, group_chans), jnp.float32)
    for offset in range(filter_taps):
        features = features + short_weight[offset] * padded[
            filter_taps - 1 - offset : filter_taps - 1 - offset + seq_rows
        ].astype(jnp.float32)
    query_part = features[:, 0]
    driven = features[:, 1] * features[:, 2]

    seg_len = seq_rows // SEGS
    poles = jnp.exp(-decay_rate)
    mode_gain = residue * jnp.sqrt(2.0 * decay_rate)
    poles_b = jnp.broadcast_to(poles[:, None, :], (modes, SEGS, group_chans))
    gains_b = jnp.broadcast_to(mode_gain[:, None, :], (modes, SEGS, group_chans))
    x_t = driven.reshape(SEGS, seg_len, group_chans).transpose(1, 0, 2)
    zero_init = jnp.zeros((modes, SEGS, group_chans), jnp.float32)
    (seg_end,) = modal_scan(x_t, poles_b, gains_b, zero_init, False)

    seg_pos = jnp.arange(SEGS, dtype=jnp.float32)
    tail_weight = jnp.exp(-decay_rate[:, None, :] * seg_len * (SEGS - 1.0 - seg_pos)[None, :, None])
    own_state = jnp.sum(tail_weight * seg_end, 1)
    blocks = lax.axis_size("ctx")
    mine = lax.axis_index("ctx")
    entering = jnp.zeros_like(own_state)
    for back in range(1, blocks):
        earlier = from_behind(own_state, "ctx", back)
        weight = jnp.exp(-decay_rate * (seq_rows * (back - 1)))
        entering = entering + jnp.where(mine >= back, weight, 0.0) * earlier
    seg_gap = seg_pos[:, None] - 1.0 - seg_pos[None, :]
    seg_mix = jnp.where(
        (seg_gap >= 0.0)[:, :, None, None],
        jnp.exp(-decay_rate[None, None] * seg_len * jnp.maximum(seg_gap, 0.0)[:, :, None, None]),
        0.0,
    )
    seg_init = jnp.einsum("jirc,ric->rjc", seg_mix, seg_end, precision=lax.Precision.HIGHEST)
    seg_init = seg_init + jnp.exp(
        -decay_rate[:, None, :] * seg_len * seg_pos[None, :, None]
    ) * entering[:, None, :]
    long_t, _ = modal_scan(x_t, poles_b, gains_b, seg_init, True)
    long_conv = long_t.transpose(1, 0, 2).reshape(seq_rows, group_chans)

    gated = (query_part * (long_conv + skip_gain * driven)).astype(jnp.bfloat16)
    gated = gated.reshape(sources, chunks, rows, group_chans)
    outs = []
    for q in range(chunks):
        rounded = jnp.einsum(
            "slc,cn->sln", gated[:, q], out_weight, preferred_element_type=jnp.float32
        ).astype(jnp.bfloat16)
        outs.append(lax.psum_scatter(rounded, "chan", scatter_dimension=0, tiled=False))
    return jnp.concatenate(outs, 0)


def solution(mesh):
    return jax.shard_map(
        local,
        mesh=mesh,
        in_specs=(
            P(("ctx", "chan"), None),
            P(None, None, "chan"),
            P(None, None, "chan"),
            P(None, "chan"),
            P(None, "chan"),
            P("chan"),
            P("chan", None),
        ),
        out_specs=P(("ctx", "chan"), None),
        check_vma=False,
    )
```

```python
import functools

import jax
import jax.numpy as jnp
from jax import lax
from jax.experimental import pallas as pl
from jax.sharding import PartitionSpec as P

SEGS = 8
LANES = 128
CHUNKS = 1


def from_behind(array, axis, by):
    size = lax.axis_size(axis)
    pairs = [(i, i + by) for i in range(size) if 0 <= i + by < size]
    return lax.ppermute(array, axis, pairs)


def scan_kernel(x_ref, p_ref, g_ref, *refs, steps, segs, with_y):
    modes = p_ref.shape[0]
    lanes = x_ref.shape[1]
    poles = [jnp.broadcast_to(p_ref[pl.ds(r, 1), :], (segs, lanes)) for r in range(modes)]
    if with_y:
        s0_ref, y_ref, end_ref = refs
        gains = [jnp.broadcast_to(g_ref[pl.ds(r, 1), :], (segs, lanes)) for r in range(modes)]
        start = tuple(s0_ref[r] for r in range(modes))
    else:
        (end_ref,) = refs
        start = tuple(jnp.zeros((segs, lanes), jnp.float32) for r in range(modes))

    def body(k, state):
        drive = x_ref[pl.ds(k, segs, stride=steps), :]
        state = tuple(poles[r] * state[r] + drive for r in range(modes))
        if with_y:
            acc = gains[0] * state[0]
            for r in range(1, modes):
                acc = acc + gains[r] * state[r]
            y_ref[pl.ds(k, segs, stride=steps), :] = acc
        return state

    state = lax.fori_loop(0, steps, body, start, unroll=2)
    for r in range(modes):
        end_ref[r] = state[r]


def modal_scan(x, poles, gains, init, with_y):
    seq_rows, chans = x.shape
    modes = poles.shape[0]
    steps = seq_rows // SEGS
    state_spec = pl.BlockSpec((modes, SEGS, LANES), lambda i: (0, 0, i))
    param_spec = pl.BlockSpec((modes, LANES), lambda i: (0, i))
    x_spec = pl.BlockSpec((seq_rows, LANES), lambda i: (0, i))
    end_shape = jax.ShapeDtypeStruct((modes, SEGS, chans), jnp.float32)
    in_specs = [x_spec, param_spec, param_spec]
    operands = [x, poles, gains]
    if with_y:
        out_shape = (jax.ShapeDtypeStruct((seq_rows, chans), jnp.float32), end_shape)
        out_specs = (x_spec, state_spec)
        in_specs.append(state_spec)
        operands.append(init)
    else:
        out_shape = (end_shape,)
        out_specs = (state_spec,)
    return pl.pallas_call(
        functools.partial(scan_kernel, steps=steps, segs=SEGS, with_y=with_y),
        grid=(chans // LANES,),
        in_specs=in_specs,
        out_specs=out_specs,
        out_shape=out_shape,
    )(*operands)


def local(tokens, in_weight, short_weight, decay_rate, residue, skip_gain, out_weight):
    group_chans = in_weight.shape[2]
    filter_taps = short_weight.shape[0]
    modes = decay_rate.shape[0]
    chunks = CHUNKS
    rows = tokens.shape[0] // chunks
    parts = []
    for q in range(chunks):
        gathered = lax.all_gather(tokens[q * rows : (q + 1) * rows], "chan", axis=0)
        parts.append(
            jnp.einsum("sld,jdc->sljc", gathered, in_weight, preferred_element_type=jnp.float32).astype(
                jnp.bfloat16
            )
        )
    sources = parts[0].shape[0]
    seq_rows = sources * chunks * rows
    projected = jnp.stack(parts, 1).reshape(seq_rows, 3, group_chans)
    tail = jnp.einsum(
        "ld,jdc->ljc", gathered[-1, rows - (filter_taps - 1) :], in_weight, preferred_element_type=jnp.float32
    ).astype(jnp.bfloat16)
    earlier_rows = from_behind(tail, "ctx", 1)
    padded = jnp.concatenate([earlier_rows, projected], 0)
    features = jnp.zeros((seq_rows, 3, group_chans), jnp.float32)
    for offset in range(filter_taps):
        features = features + short_weight[offset] * padded[
            filter_taps - 1 - offset : filter_taps - 1 - offset + seq_rows
        ].astype(jnp.float32)
    query_part = features[:, 0]
    driven = features[:, 1] * features[:, 2]

    seg_len = seq_rows // SEGS
    poles = jnp.exp(-decay_rate)
    mode_gain = residue * jnp.sqrt(2.0 * decay_rate)
    (seg_end,) = modal_scan(driven, poles, mode_gain, None, False)

    seg_pos = jnp.arange(SEGS, dtype=jnp.float32)
    tail_weight = jnp.exp(-decay_rate[:, None, :] * seg_len * (SEGS - 1.0 - seg_pos)[None, :, None])
    own_state = jnp.sum(tail_weight * seg_end, 1)
    blocks = lax.axis_size("ctx")
    mine = lax.axis_index("ctx")
    entering = jnp.zeros_like(own_state)
    for back in range(1, blocks):
        earlier = from_behind(own_state, "ctx", back)
        weight = jnp.exp(-decay_rate * (seq_rows * (back - 1)))
        entering = entering + jnp.where(mine >= back, weight, 0.0) * earlier
    seg_gap = seg_pos[:, None] - 1.0 - seg_pos[None, :]
    seg_mix = jnp.where(
        (seg_gap >= 0.0)[:, :, None, None],
        jnp.exp(-decay_rate[None, None] * seg_len * jnp.maximum(seg_gap, 0.0)[:, :, None, None]),
        0.0,
    )
    seg_init = jnp.einsum("jirc,ric->rjc", seg_mix, seg_end, precision=lax.Precision.HIGHEST)
    seg_init = seg_init + jnp.exp(
        -decay_rate[:, None, :] * seg_len * seg_pos[None, :, None]
    ) * entering[:, None, :]
    long_conv, _ = modal_scan(driven, poles, mode_gain, seg_init, True)

    gated = (query_part * (long_conv + skip_gain * driven)).astype(jnp.bfloat16)
    gated = gated.reshape(sources, chunks, rows, group_chans)
    outs = []
    for q in range(chunks):
        rounded = jnp.einsum(
            "slc,cn->sln", gated[:, q], out_weight, preferred_element_type=jnp.float32
        ).astype(jnp.bfloat16)
        outs.append(lax.psum_scatter(rounded, "chan", scatter_dimension=0, tiled=False))
    return jnp.concatenate(outs, 0)


def solution(mesh):
    return jax.shard_map(
        local,
        mesh=mesh,
        in_specs=(
            P(("ctx", "chan"), None),
            P(None, None, "chan"),
            P(None, None, "chan"),
            P(None, "chan"),
            P(None, "chan"),
            P("chan"),
            P("chan", None),
        ),
        out_specs=P(("ctx", "chan"), None),
        check_vma=False,
    )
```

```python
import functools

import jax
import jax.numpy as jnp
from jax import lax
from jax.experimental import pallas as pl
from jax.sharding import PartitionSpec as P

SEGS = 8
LANES = 128
CHUNKS = 1


def from_behind(array, axis, by):
    size = lax.axis_size(axis)
    pairs = [(i, i + by) for i in range(size) if 0 <= i + by < size]
    return lax.ppermute(array, axis, pairs)


def scan_kernel(x_ref, p_ref, g_ref, *refs, steps, segs, with_y):
    modes = p_ref.shape[0]
    lanes = x_ref.shape[1]
    poles = [jnp.broadcast_to(p_ref[pl.ds(r, 1), :], (segs, lanes)) for r in range(modes)]
    if with_y:
        q_ref, skip_ref, s0_ref, y_ref, end_ref = refs
        skip = jnp.broadcast_to(skip_ref[...], (segs, lanes))
        gains = [jnp.broadcast_to(g_ref[pl.ds(r, 1), :], (segs, lanes)) for r in range(modes)]
        start = tuple(s0_ref[r] for r in range(modes))
    else:
        (end_ref,) = refs
        start = tuple(jnp.zeros((segs, lanes), jnp.float32) for r in range(modes))

    def body(k, state):
        drive = x_ref[pl.ds(k, segs, stride=steps), :]
        state = tuple(poles[r] * state[r] + drive for r in range(modes))
        if with_y:
            acc = gains[0] * state[0]
            for r in range(1, modes):
                acc = acc + gains[r] * state[r]
            rows = pl.ds(k, segs, stride=steps)
            y_ref[rows, :] = q_ref[rows, :] * (acc + skip * drive)
        return state

    state = lax.fori_loop(0, steps, body, start, unroll=2)
    for r in range(modes):
        end_ref[r] = state[r]


def modal_scan(x, poles, gains, init, with_y, query=None, skip=None):
    seq_rows, chans = x.shape
    modes = poles.shape[0]
    steps = seq_rows // SEGS
    state_spec = pl.BlockSpec((modes, SEGS, LANES), lambda i: (0, 0, i))
    param_spec = pl.BlockSpec((modes, LANES), lambda i: (0, i))
    x_spec = pl.BlockSpec((seq_rows, LANES), lambda i: (0, i))
    end_shape = jax.ShapeDtypeStruct((modes, SEGS, chans), jnp.float32)
    in_specs = [x_spec, param_spec, param_spec]
    operands = [x, poles, gains]
    if with_y:
        out_shape = (jax.ShapeDtypeStruct((seq_rows, chans), jnp.float32), end_shape)
        out_specs = (x_spec, state_spec)
        in_specs += [x_spec, pl.BlockSpec((1, LANES), lambda i: (0, i)), state_spec]
        operands += [query, skip.reshape(1, chans), init]
    else:
        out_shape = (end_shape,)
        out_specs = (state_spec,)
    return pl.pallas_call(
        functools.partial(scan_kernel, steps=steps, segs=SEGS, with_y=with_y),
        grid=(chans // LANES,),
        in_specs=in_specs,
        out_specs=out_specs,
        out_shape=out_shape,
    )(*operands)


def local(tokens, in_weight, short_weight, decay_rate, residue, skip_gain, out_weight):
    group_chans = in_weight.shape[2]
    filter_taps = short_weight.shape[0]
    modes = decay_rate.shape[0]
    chunks = CHUNKS
    rows = tokens.shape[0] // chunks
    parts = []
    for q in range(chunks):
        gathered = lax.all_gather(tokens[q * rows : (q + 1) * rows], "chan", axis=0)
        parts.append(
            jnp.einsum("sld,jdc->sljc", gathered, in_weight, preferred_element_type=jnp.float32).astype(
                jnp.bfloat16
            )
        )
    sources = parts[0].shape[0]
    seq_rows = sources * chunks * rows
    projected = jnp.stack(parts, 1).reshape(seq_rows, 3, group_chans)
    tail = jnp.einsum(
        "ld,jdc->ljc", gathered[-1, rows - (filter_taps - 1) :], in_weight, preferred_element_type=jnp.float32
    ).astype(jnp.bfloat16)
    earlier_rows = from_behind(tail, "ctx", 1)
    padded = jnp.concatenate([earlier_rows, projected], 0)
    features = jnp.zeros((seq_rows, 3, group_chans), jnp.float32)
    for offset in range(filter_taps):
        features = features + short_weight[offset] * padded[
            filter_taps - 1 - offset : filter_taps - 1 - offset + seq_rows
        ].astype(jnp.float32)
    query_part = features[:, 0]
    driven = features[:, 1] * features[:, 2]

    seg_len = seq_rows // SEGS
    poles = jnp.exp(-decay_rate)
    mode_gain = residue * jnp.sqrt(2.0 * decay_rate)
    (seg_end,) = modal_scan(driven, poles, mode_gain, None, False)

    seg_pos = jnp.arange(SEGS, dtype=jnp.float32)
    tail_weight = jnp.exp(-decay_rate[:, None, :] * seg_len * (SEGS - 1.0 - seg_pos)[None, :, None])
    own_state = jnp.sum(tail_weight * seg_end, 1)
    blocks = lax.axis_size("ctx")
    mine = lax.axis_index("ctx")
    placed = jnp.where((jnp.arange(blocks) == mine)[:, None, None], own_state[None], 0.0)
    states = lax.psum(placed, "ctx")
    back = (mine - 1 - jnp.arange(blocks)).astype(jnp.float32)
    block_weight = jnp.where(
        (back >= 0.0)[:, None, None],
        jnp.exp(-decay_rate[None] * seq_rows * jnp.maximum(back, 0.0)[:, None, None]),
        0.0,
    )
    entering = jnp.sum(block_weight * states, 0)
    seg_gap = seg_pos[:, None] - 1.0 - seg_pos[None, :]
    seg_mix = jnp.where(
        (seg_gap >= 0.0)[:, :, None, None],
        jnp.exp(-decay_rate[None, None] * seg_len * jnp.maximum(seg_gap, 0.0)[:, :, None, None]),
        0.0,
    )
    seg_init = jnp.einsum("jirc,ric->rjc", seg_mix, seg_end, precision=lax.Precision.HIGHEST)
    seg_init = seg_init + jnp.exp(
        -decay_rate[:, None, :] * seg_len * seg_pos[None, :, None]
    ) * entering[:, None, :]
    gated, _ = modal_scan(driven, poles, mode_gain, seg_init, True, query_part, skip_gain)
    gated = gated.astype(jnp.bfloat16)
    gated = gated.reshape(sources, chunks, rows, group_chans)
    outs = []
    for q in range(chunks):
        rounded = jnp.einsum(
            "slc,cn->sln", gated[:, q], out_weight, preferred_element_type=jnp.float32
        ).astype(jnp.bfloat16)
        outs.append(lax.psum_scatter(rounded, "chan", scatter_dimension=0, tiled=False))
    return jnp.concatenate(outs, 0)


def solution(mesh):
    return jax.shard_map(
        local,
        mesh=mesh,
        in_specs=(
            P(("ctx", "chan"), None),
            P(None, None, "chan"),
            P(None, None, "chan"),
            P(None, "chan"),
            P(None, "chan"),
            P("chan"),
            P("chan", None),
        ),
        out_specs=P(("ctx", "chan"), None),
        check_vma=False,
    )
```

```python
import functools

import jax
import jax.numpy as jnp
from jax import lax
from jax.experimental import pallas as pl
from jax.sharding import PartitionSpec as P

SEGS = 8
LANES = 128
CHUNKS = 1


def from_behind(array, axis, by):
    size = lax.axis_size(axis)
    pairs = [(i, i + by) for i in range(size) if 0 <= i + by < size]
    return lax.ppermute(array, axis, pairs)


def scan_kernel(x_ref, p_ref, g_ref, *refs, steps, segs, with_y):
    modes = p_ref.shape[0]
    lanes = x_ref.shape[1]
    poles = [jnp.broadcast_to(p_ref[pl.ds(r, 1), :], (segs, lanes)) for r in range(modes)]
    if with_y:
        q_ref, skip_ref, s0_ref, y_ref, end_ref = refs
        skip = jnp.broadcast_to(skip_ref[...], (segs, lanes))
        gains = [jnp.broadcast_to(g_ref[pl.ds(r, 1), :], (segs, lanes)) for r in range(modes)]
        start = tuple(s0_ref[r] for r in range(modes))
    else:
        (end_ref,) = refs
        start = tuple(jnp.zeros((segs, lanes), jnp.float32) for r in range(modes))

    def body(k, state):
        drive = x_ref[pl.ds(k, segs, stride=steps), :]
        state = tuple(poles[r] * state[r] + drive for r in range(modes))
        if with_y:
            acc = gains[0] * state[0]
            for r in range(1, modes):
                acc = acc + gains[r] * state[r]
            rows = pl.ds(k, segs, stride=steps)
            y_ref[rows, :] = q_ref[rows, :] * (acc + skip * drive)
        return state

    state = lax.fori_loop(0, steps, body, start, unroll=2)
    for r in range(modes):
        end_ref[r] = state[r]


def modal_scan(x, poles, gains, init, with_y, query=None, skip=None):
    seq_rows, chans = x.shape
    modes = poles.shape[0]
    steps = seq_rows // SEGS
    state_spec = pl.BlockSpec((modes, SEGS, LANES), lambda i: (0, 0, i))
    param_spec = pl.BlockSpec((modes, LANES), lambda i: (0, i))
    x_spec = pl.BlockSpec((seq_rows, LANES), lambda i: (0, i))
    end_shape = jax.ShapeDtypeStruct((modes, SEGS, chans), jnp.float32)
    in_specs = [x_spec, param_spec, param_spec]
    operands = [x, poles, gains]
    if with_y:
        out_shape = (jax.ShapeDtypeStruct((seq_rows, chans), jnp.float32), end_shape)
        out_specs = (x_spec, state_spec)
        in_specs += [x_spec, pl.BlockSpec((1, LANES), lambda i: (0, i)), state_spec]
        operands += [query, skip.reshape(1, chans), init]
    else:
        out_shape = (end_shape,)
        out_specs = (state_spec,)
    return pl.pallas_call(
        functools.partial(scan_kernel, steps=steps, segs=SEGS, with_y=with_y),
        grid=(chans // LANES,),
        in_specs=in_specs,
        out_specs=out_specs,
        out_shape=out_shape,
    )(*operands)


def local(tokens, in_weight, short_weight, decay_rate, residue, skip_gain, out_weight):
    group_chans = in_weight.shape[2]
    filter_taps = short_weight.shape[0]
    modes = decay_rate.shape[0]
    chunks = CHUNKS
    rows = tokens.shape[0] // chunks
    parts = []
    for q in range(chunks):
        gathered = lax.all_gather(tokens[q * rows : (q + 1) * rows], "chan", axis=0)
        parts.append(
            jnp.einsum("sld,jdc->sljc", gathered, in_weight, preferred_element_type=jnp.float32).astype(
                jnp.bfloat16
            )
        )
    sources = parts[0].shape[0]
    seq_rows = sources * chunks * rows
    projected = jnp.stack(parts, 1).reshape(seq_rows, 3, group_chans)
    tail = jnp.einsum(
        "ld,jdc->ljc", gathered[-1, rows - (filter_taps - 1) :], in_weight, preferred_element_type=jnp.float32
    ).astype(jnp.bfloat16)
    earlier_rows = from_behind(tail, "ctx", 1)
    padded = jnp.concatenate([earlier_rows, projected], 0)
    features = jnp.zeros((seq_rows, 3, group_chans), jnp.float32)
    for offset in range(filter_taps):
        features = features + short_weight[offset] * padded[
            filter_taps - 1 - offset : filter_taps - 1 - offset + seq_rows
        ].astype(jnp.float32)
    query_part = features[:, 0]
    driven = features[:, 1] * features[:, 2]

    seg_len = seq_rows // SEGS
    poles = jnp.exp(-decay_rate)
    mode_gain = residue * jnp.sqrt(2.0 * decay_rate)
    (seg_end,) = modal_scan(driven, poles, mode_gain, None, False)

    seg_pos = jnp.arange(SEGS, dtype=jnp.float32)
    tail_weight = jnp.exp(-decay_rate[:, None, :] * seg_len * (SEGS - 1.0 - seg_pos)[None, :, None])
    own_state = jnp.sum(tail_weight * seg_end, 1)
    blocks = lax.axis_size("ctx")
    mine = lax.axis_index("ctx")
    entering = jnp.zeros_like(own_state)
    for back in range(1, blocks):
        earlier = from_behind(own_state, "ctx", back)
        weight = jnp.exp(-decay_rate * (seq_rows * (back - 1)))
        entering = entering + jnp.where(mine >= back, weight, 0.0) * earlier
    seg_gap = seg_pos[:, None] - 1.0 - seg_pos[None, :]
    seg_mix = jnp.where(
        (seg_gap >= 0.0)[:, :, None, None],
        jnp.exp(-decay_rate[None, None] * seg_len * jnp.maximum(seg_gap, 0.0)[:, :, None, None]),
        0.0,
    )
    seg_init = jnp.einsum("jirc,ric->rjc", seg_mix, seg_end, precision=lax.Precision.HIGHEST)
    seg_init = seg_init + jnp.exp(
        -decay_rate[:, None, :] * seg_len * seg_pos[None, :, None]
    ) * entering[:, None, :]
    gated, _ = modal_scan(driven, poles, mode_gain, seg_init, True, query_part, skip_gain)
    gated = gated.astype(jnp.bfloat16)
    gated = gated.reshape(sources, chunks, rows, group_chans)
    outs = []
    for q in range(chunks):
        rounded = jnp.einsum(
            "slc,cn->sln", gated[:, q], out_weight, preferred_element_type=jnp.float32
        ).astype(jnp.bfloat16)
        received = lax.all_to_all(rounded, "chan", 0, 0)
        outs.append(jnp.sum(received.astype(jnp.float32), 0).astype(jnp.bfloat16))
    return jnp.concatenate(outs, 0)


def solution(mesh):
    return jax.shard_map(
        local,
        mesh=mesh,
        in_specs=(
            P(("ctx", "chan"), None),
            P(None, None, "chan"),
            P(None, None, "chan"),
            P(None, "chan"),
            P(None, "chan"),
            P("chan"),
            P("chan", None),
        ),
        out_specs=P(("ctx", "chan"), None),
        check_vma=False,
    )
```

```python
import functools

import jax
import jax.numpy as jnp
from jax import lax
from jax.experimental import pallas as pl
from jax.sharding import PartitionSpec as P

SEGS = 8
LANES = 128
CHUNKS = 1


def from_behind(array, axis, by):
    size = lax.axis_size(axis)
    pairs = [(i, i + by) for i in range(size) if 0 <= i + by < size]
    return lax.ppermute(array, axis, pairs)


def scan_kernel(x_ref, p_ref, g_ref, *refs, steps, segs, with_y):
    modes = p_ref.shape[0]
    lanes = x_ref.shape[1]
    poles = [jnp.broadcast_to(p_ref[pl.ds(r, 1), :], (segs, lanes)) for r in range(modes)]
    if with_y:
        q_ref, skip_ref, s0_ref, y_ref, end_ref = refs
        skip = jnp.broadcast_to(skip_ref[...], (segs, lanes))
        gains = [jnp.broadcast_to(g_ref[pl.ds(r, 1), :], (segs, lanes)) for r in range(modes)]
        start = tuple(s0_ref[r] for r in range(modes))
    else:
        (end_ref,) = refs
        start = tuple(jnp.zeros((segs, lanes), jnp.float32) for r in range(modes))

    def body(k, state):
        drive = x_ref[pl.ds(k, segs, stride=steps), :]
        state = tuple(poles[r] * state[r] + drive for r in range(modes))
        if with_y:
            acc = gains[0] * state[0]
            for r in range(1, modes):
                acc = acc + gains[r] * state[r]
            rows = pl.ds(k, segs, stride=steps)
            y_ref[rows, :] = q_ref[rows, :] * (acc + skip * drive)
        return state

    state = lax.fori_loop(0, steps, body, start, unroll=8)
    for r in range(modes):
        end_ref[r] = state[r]


def modal_scan(x, poles, gains, init, with_y, query=None, skip=None):
    seq_rows, chans = x.shape
    modes = poles.shape[0]
    steps = seq_rows // SEGS
    state_spec = pl.BlockSpec((modes, SEGS, LANES), lambda i: (0, 0, i))
    param_spec = pl.BlockSpec((modes, LANES), lambda i: (0, i))
    x_spec = pl.BlockSpec((seq_rows, LANES), lambda i: (0, i))
    end_shape = jax.ShapeDtypeStruct((modes, SEGS, chans), jnp.float32)
    in_specs = [x_spec, param_spec, param_spec]
    operands = [x, poles, gains]
    if with_y:
        out_shape = (jax.ShapeDtypeStruct((seq_rows, chans), jnp.float32), end_shape)
        out_specs = (x_spec, state_spec)
        in_specs += [x_spec, pl.BlockSpec((1, LANES), lambda i: (0, i)), state_spec]
        operands += [query, skip.reshape(1, chans), init]
    else:
        out_shape = (end_shape,)
        out_specs = (state_spec,)
    return pl.pallas_call(
        functools.partial(scan_kernel, steps=steps, segs=SEGS, with_y=with_y),
        grid=(chans // LANES,),
        in_specs=in_specs,
        out_specs=out_specs,
        out_shape=out_shape,
    )(*operands)


def local(tokens, in_weight, short_weight, decay_rate, residue, skip_gain, out_weight):
    group_chans = in_weight.shape[2]
    filter_taps = short_weight.shape[0]
    modes = decay_rate.shape[0]
    chunks = CHUNKS
    rows = tokens.shape[0] // chunks
    parts = []
    for q in range(chunks):
        gathered = lax.all_gather(tokens[q * rows : (q + 1) * rows], "chan", axis=0)
        parts.append(
            jnp.einsum("sld,jdc->sljc", gathered, in_weight, preferred_element_type=jnp.float32).astype(
                jnp.bfloat16
            )
        )
    sources = parts[0].shape[0]
    seq_rows = sources * chunks * rows
    projected = jnp.stack(parts, 1).reshape(seq_rows, 3, group_chans)
    tail = jnp.einsum(
        "ld,jdc->ljc", gathered[-1, rows - (filter_taps - 1) :], in_weight, preferred_element_type=jnp.float32
    ).astype(jnp.bfloat16)
    earlier_rows = from_behind(tail, "ctx", 1)
    padded = jnp.concatenate([earlier_rows, projected], 0)
    features = jnp.zeros((seq_rows, 3, group_chans), jnp.float32)
    for offset in range(filter_taps):
        features = features + short_weight[offset] * padded[
            filter_taps - 1 - offset : filter_taps - 1 - offset + seq_rows
        ].astype(jnp.float32)
    query_part = features[:, 0]
    driven = features[:, 1] * features[:, 2]

    seg_len = seq_rows // SEGS
    poles = jnp.exp(-decay_rate)
    mode_gain = residue * jnp.sqrt(2.0 * decay_rate)
    (seg_end,) = modal_scan(driven, poles, mode_gain, None, False)

    seg_pos = jnp.arange(SEGS, dtype=jnp.float32)
    tail_weight = jnp.exp(-decay_rate[:, None, :] * seg_len * (SEGS - 1.0 - seg_pos)[None, :, None])
    own_state = jnp.sum(tail_weight * seg_end, 1)
    blocks = lax.axis_size("ctx")
    mine = lax.axis_index("ctx")
    entering = jnp.zeros_like(own_state)
    for back in range(1, blocks):
        earlier = from_behind(own_state, "ctx", back)
        weight = jnp.exp(-decay_rate * (seq_rows * (back - 1)))
        entering = entering + jnp.where(mine >= back, weight, 0.0) * earlier
    seg_gap = seg_pos[:, None] - 1.0 - seg_pos[None, :]
    seg_mix = jnp.where(
        (seg_gap >= 0.0)[:, :, None, None],
        jnp.exp(-decay_rate[None, None] * seg_len * jnp.maximum(seg_gap, 0.0)[:, :, None, None]),
        0.0,
    )
    seg_init = jnp.einsum("jirc,ric->rjc", seg_mix, seg_end, precision=lax.Precision.HIGHEST)
    seg_init = seg_init + jnp.exp(
        -decay_rate[:, None, :] * seg_len * seg_pos[None, :, None]
    ) * entering[:, None, :]
    gated, _ = modal_scan(driven, poles, mode_gain, seg_init, True, query_part, skip_gain)
    gated = gated.astype(jnp.bfloat16)
    gated = gated.reshape(sources, chunks, rows, group_chans)
    outs = []
    for q in range(chunks):
        rounded = jnp.einsum(
            "slc,cn->sln", gated[:, q], out_weight, preferred_element_type=jnp.float32
        ).astype(jnp.bfloat16)
        outs.append(lax.psum_scatter(rounded, "chan", scatter_dimension=0, tiled=False))
    return jnp.concatenate(outs, 0)


def solution(mesh):
    return jax.shard_map(
        local,
        mesh=mesh,
        in_specs=(
            P(("ctx", "chan"), None),
            P(None, None, "chan"),
            P(None, None, "chan"),
            P(None, "chan"),
            P(None, "chan"),
            P("chan"),
            P("chan", None),
        ),
        out_specs=P(("ctx", "chan"), None),
        check_vma=False,
    )
```

```python
import functools

import jax
import jax.numpy as jnp
from jax import lax
from jax.experimental import pallas as pl
from jax.sharding import PartitionSpec as P

SEGS = 8
LANES = 128
CHUNKS = 1


def from_behind(array, axis, by):
    size = lax.axis_size(axis)
    pairs = [(i, i + by) for i in range(size) if 0 <= i + by < size]
    return lax.ppermute(array, axis, pairs)


def scan_kernel(x_ref, p_ref, g_ref, *refs, steps, segs, with_y):
    modes = p_ref.shape[0]
    lanes = x_ref.shape[1]
    poles = [jnp.broadcast_to(p_ref[pl.ds(r, 1), :], (segs, lanes)) for r in range(modes)]
    if with_y:
        q_ref, skip_ref, s0_ref, y_ref, end_ref = refs
        skip = jnp.broadcast_to(skip_ref[...], (segs, lanes))
        gains = [jnp.broadcast_to(g_ref[pl.ds(r, 1), :], (segs, lanes)) for r in range(modes)]
        start = tuple(s0_ref[r] for r in range(modes))
    else:
        (end_ref,) = refs
        start = tuple(jnp.zeros((segs, lanes), jnp.float32) for r in range(modes))

    def body(k, state):
        drive = x_ref[pl.ds(k, segs, stride=steps), :]
        state = tuple(poles[r] * state[r] + drive for r in range(modes))
        if with_y:
            acc = gains[0] * state[0]
            for r in range(1, modes):
                acc = acc + gains[r] * state[r]
            rows = pl.ds(k, segs, stride=steps)
            y_ref[rows, :] = q_ref[rows, :] * (acc + skip * drive)
        return state

    state = lax.fori_loop(0, steps, body, start, unroll=8)
    for r in range(modes):
        end_ref[r] = state[r]


def modal_scan(x, poles, gains, init, with_y, query=None, skip=None):
    seq_rows, chans = x.shape
    modes = poles.shape[0]
    steps = seq_rows // SEGS
    state_spec = pl.BlockSpec((modes, SEGS, LANES), lambda i: (0, 0, i))
    param_spec = pl.BlockSpec((modes, LANES), lambda i: (0, i))
    x_spec = pl.BlockSpec((seq_rows, LANES), lambda i: (0, i))
    end_shape = jax.ShapeDtypeStruct((modes, SEGS, chans), jnp.float32)
    in_specs = [x_spec, param_spec, param_spec]
    operands = [x, poles, gains]
    if with_y:
        out_shape = (jax.ShapeDtypeStruct((seq_rows, chans), jnp.float32), end_shape)
        out_specs = (x_spec, state_spec)
        in_specs += [x_spec, pl.BlockSpec((1, LANES), lambda i: (0, i)), state_spec]
        operands += [query, skip.reshape(1, chans), init]
    else:
        out_shape = (end_shape,)
        out_specs = (state_spec,)
    return pl.pallas_call(
        functools.partial(scan_kernel, steps=steps, segs=SEGS, with_y=with_y),
        grid=(chans // LANES,),
        in_specs=in_specs,
        out_specs=out_specs,
        out_shape=out_shape,
    )(*operands)


def carry_kernel(p_ref, q_ref, part_ref, c0_ref, out_ref, *, steps, segs):
    modes = p_ref.shape[0]
    lanes = q_ref.shape[1]
    poles = [jnp.broadcast_to(p_ref[pl.ds(r, 1), :], (segs, lanes)) for r in range(modes)]

    def body(k, carry):
        carry = tuple(poles[r] * carry[r] for r in range(modes))
        acc = carry[0]
        for r in range(1, modes):
            acc = acc + carry[r]
        rows = pl.ds(k, segs, stride=steps)
        out_ref[rows, :] = part_ref[rows, :] + q_ref[rows, :] * acc
        return carry

    lax.fori_loop(0, steps, body, tuple(c0_ref[r] for r in range(modes)), unroll=8)


def add_carried(poles, query, partial, start):
    seq_rows, chans = query.shape
    modes = poles.shape[0]
    row_spec = pl.BlockSpec((seq_rows, LANES), lambda i: (0, i))
    return pl.pallas_call(
        functools.partial(carry_kernel, steps=seq_rows // SEGS, segs=SEGS),
        grid=(chans // LANES,),
        in_specs=[
            pl.BlockSpec((modes, LANES), lambda i: (0, i)),
            row_spec,
            row_spec,
            pl.BlockSpec((modes, SEGS, LANES), lambda i: (0, 0, i)),
        ],
        out_specs=row_spec,
        out_shape=jax.ShapeDtypeStruct((seq_rows, chans), jnp.float32),
    )(poles, query, partial, start)


def local(tokens, in_weight, short_weight, decay_rate, residue, skip_gain, out_weight):
    group_chans = in_weight.shape[2]
    filter_taps = short_weight.shape[0]
    modes = decay_rate.shape[0]
    chunks = CHUNKS
    rows = tokens.shape[0] // chunks
    parts = []
    for q in range(chunks):
        gathered = lax.all_gather(tokens[q * rows : (q + 1) * rows], "chan", axis=0)
        parts.append(
            jnp.einsum("sld,jdc->sljc", gathered, in_weight, preferred_element_type=jnp.float32).astype(
                jnp.bfloat16
            )
        )
    sources = parts[0].shape[0]
    seq_rows = sources * chunks * rows
    projected = jnp.stack(parts, 1).reshape(seq_rows, 3, group_chans)
    tail = jnp.einsum(
        "ld,jdc->ljc", gathered[-1, rows - (filter_taps - 1) :], in_weight, preferred_element_type=jnp.float32
    ).astype(jnp.bfloat16)
    earlier_rows = from_behind(tail, "ctx", 1)
    padded = jnp.concatenate([earlier_rows, projected], 0)
    features = jnp.zeros((seq_rows, 3, group_chans), jnp.float32)
    for offset in range(filter_taps):
        features = features + short_weight[offset] * padded[
            filter_taps - 1 - offset : filter_taps - 1 - offset + seq_rows
        ].astype(jnp.float32)
    query_part = features[:, 0]
    driven = features[:, 1] * features[:, 2]

    seg_len = seq_rows // SEGS
    poles = jnp.exp(-decay_rate)
    mode_gain = residue * jnp.sqrt(2.0 * decay_rate)
    (seg_end,) = modal_scan(driven, poles, mode_gain, None, False)

    seg_pos = jnp.arange(SEGS, dtype=jnp.float32)
    tail_weight = jnp.exp(-decay_rate[:, None, :] * seg_len * (SEGS - 1.0 - seg_pos)[None, :, None])
    own_state = jnp.sum(tail_weight * seg_end, 1)
    blocks = lax.axis_size("ctx")
    mine = lax.axis_index("ctx")
    entering = jnp.zeros_like(own_state)
    for back in range(1, blocks):
        earlier = from_behind(own_state, "ctx", back)
        weight = jnp.exp(-decay_rate * (seq_rows * (back - 1)))
        entering = entering + jnp.where(mine >= back, weight, 0.0) * earlier
    seg_gap = seg_pos[:, None] - 1.0 - seg_pos[None, :]
    seg_mix = jnp.where(
        (seg_gap >= 0.0)[:, :, None, None],
        jnp.exp(-decay_rate[None, None] * seg_len * jnp.maximum(seg_gap, 0.0)[:, :, None, None]),
        0.0,
    )
    seg_init = jnp.einsum("jirc,ric->rjc", seg_mix, seg_end, precision=lax.Precision.HIGHEST)
    gated, _ = modal_scan(driven, poles, mode_gain, seg_init, True, query_part, skip_gain)
    carried = mode_gain[:, None, :] * jnp.exp(
        -decay_rate[:, None, :] * seg_len * seg_pos[None, :, None]
    ) * entering[:, None, :]
    gated = add_carried(poles, query_part, gated, carried)
    gated = gated.astype(jnp.bfloat16)
    gated = gated.reshape(sources, chunks, rows, group_chans)
    outs = []
    for q in range(chunks):
        rounded = jnp.einsum(
            "slc,cn->sln", gated[:, q], out_weight, preferred_element_type=jnp.float32
        ).astype(jnp.bfloat16)
        outs.append(lax.psum_scatter(rounded, "chan", scatter_dimension=0, tiled=False))
    return jnp.concatenate(outs, 0)


def solution(mesh):
    return jax.shard_map(
        local,
        mesh=mesh,
        in_specs=(
            P(("ctx", "chan"), None),
            P(None, None, "chan"),
            P(None, None, "chan"),
            P(None, "chan"),
            P(None, "chan"),
            P("chan"),
            P("chan", None),
        ),
        out_specs=P(("ctx", "chan"), None),
        check_vma=False,
    )
```

```python
import functools

import jax
import jax.numpy as jnp
from jax import lax
from jax.experimental import pallas as pl
from jax.sharding import PartitionSpec as P

SEGS = 8
LANES = 128
CHUNKS = 1


def from_behind(array, axis, by):
    size = lax.axis_size(axis)
    pairs = [(i, i + by) for i in range(size) if 0 <= i + by < size]
    return lax.ppermute(array, axis, pairs)


def scan_kernel(x_ref, p_ref, g_ref, *refs, steps, segs, with_y):
    modes = p_ref.shape[0]
    lanes = x_ref.shape[1]
    poles = [jnp.broadcast_to(p_ref[pl.ds(r, 1), :], (segs, lanes)) for r in range(modes)]
    if with_y:
        q_ref, skip_ref, s0_ref, y_ref, end_ref = refs
        skip = jnp.broadcast_to(skip_ref[...], (segs, lanes))
        gains = [jnp.broadcast_to(g_ref[pl.ds(r, 1), :], (segs, lanes)) for r in range(modes)]
        start = tuple(s0_ref[r] for r in range(modes))
    else:
        (end_ref,) = refs
        start = tuple(jnp.zeros((segs, lanes), jnp.float32) for r in range(modes))

    def body(k, state):
        drive = x_ref[pl.ds(k, segs, stride=steps), :]
        state = tuple(poles[r] * state[r] + drive for r in range(modes))
        if with_y:
            acc = gains[0] * state[0]
            for r in range(1, modes):
                acc = acc + gains[r] * state[r]
            rows = pl.ds(k, segs, stride=steps)
            y_ref[rows, :] = q_ref[rows, :] * (acc + skip * drive)
        return state

    state = lax.fori_loop(0, steps, body, start, unroll=8)
    for r in range(modes):
        end_ref[r] = state[r]


def modal_scan(x, poles, gains, init, with_y, query=None, skip=None):
    seq_rows, chans = x.shape
    modes = poles.shape[0]
    steps = seq_rows // SEGS
    state_spec = pl.BlockSpec((modes, SEGS, LANES), lambda i: (0, 0, i))
    param_spec = pl.BlockSpec((modes, LANES), lambda i: (0, i))
    x_spec = pl.BlockSpec((seq_rows, LANES), lambda i: (0, i))
    end_shape = jax.ShapeDtypeStruct((modes, SEGS, chans), jnp.float32)
    in_specs = [x_spec, param_spec, param_spec]
    operands = [x, poles, gains]
    if with_y:
        out_shape = (jax.ShapeDtypeStruct((seq_rows, chans), jnp.float32), end_shape)
        out_specs = (x_spec, state_spec)
        in_specs += [x_spec, pl.BlockSpec((1, LANES), lambda i: (0, i)), state_spec]
        operands += [query, skip.reshape(1, chans), init]
    else:
        out_shape = (end_shape,)
        out_specs = (state_spec,)
    return pl.pallas_call(
        functools.partial(scan_kernel, steps=steps, segs=SEGS, with_y=with_y),
        grid=(chans // LANES,),
        in_specs=in_specs,
        out_specs=out_specs,
        out_shape=out_shape,
    )(*operands)


def carry_kernel(p_ref, q_ref, part_ref, c0_ref, out_ref, *, steps, segs):
    modes = p_ref.shape[0]
    lanes = q_ref.shape[1]
    poles = [jnp.broadcast_to(p_ref[pl.ds(r, 1), :], (segs, lanes)) for r in range(modes)]

    def body(k, carry):
        carry = tuple(poles[r] * carry[r] for r in range(modes))
        acc = carry[0]
        for r in range(1, modes):
            acc = acc + carry[r]
        rows = pl.ds(k, segs, stride=steps)
        out_ref[rows, :] = part_ref[rows, :] + q_ref[rows, :] * acc
        return carry

    lax.fori_loop(0, steps, body, tuple(c0_ref[r] for r in range(modes)), unroll=8)


def add_carried(poles, query, partial, start):
    seq_rows, chans = query.shape
    modes = poles.shape[0]
    row_spec = pl.BlockSpec((seq_rows, LANES), lambda i: (0, i))
    return pl.pallas_call(
        functools.partial(carry_kernel, steps=seq_rows // SEGS, segs=SEGS),
        grid=(chans // LANES,),
        in_specs=[
            pl.BlockSpec((modes, LANES), lambda i: (0, i)),
            row_spec,
            row_spec,
            pl.BlockSpec((modes, SEGS, LANES), lambda i: (0, 0, i)),
        ],
        out_specs=row_spec,
        out_shape=jax.ShapeDtypeStruct((seq_rows, chans), jnp.float32),
    )(poles, query, partial, start)


def local(tokens, in_weight, short_weight, decay_rate, residue, skip_gain, out_weight):
    group_chans = in_weight.shape[2]
    filter_taps = short_weight.shape[0]
    modes = decay_rate.shape[0]
    chunks = CHUNKS
    rows = tokens.shape[0] // chunks
    parts = []
    for q in range(chunks):
        gathered = lax.all_gather(tokens[q * rows : (q + 1) * rows], "chan", axis=0)
        parts.append(
            jnp.einsum("sld,jdc->sljc", gathered, in_weight, preferred_element_type=jnp.float32).astype(
                jnp.bfloat16
            )
        )
    sources = parts[0].shape[0]
    seq_rows = sources * chunks * rows
    projected = jnp.stack(parts, 1).reshape(seq_rows, 3, group_chans)
    tail = jnp.einsum(
        "ld,jdc->ljc", gathered[-1, rows - (filter_taps - 1) :], in_weight, preferred_element_type=jnp.float32
    ).astype(jnp.bfloat16)
    earlier_rows = from_behind(tail, "ctx", 1)
    padded = jnp.concatenate([earlier_rows, projected], 0)
    features = jnp.zeros((seq_rows, 3, group_chans), jnp.float32)
    for offset in range(filter_taps):
        features = features + short_weight[offset] * padded[
            filter_taps - 1 - offset : filter_taps - 1 - offset + seq_rows
        ].astype(jnp.float32)
    query_part = features[:, 0]
    driven = features[:, 1] * features[:, 2]

    seg_len = seq_rows // SEGS
    poles = jnp.exp(-decay_rate)
    mode_gain = residue * jnp.sqrt(2.0 * decay_rate)
    (seg_end,) = modal_scan(driven, poles, mode_gain, None, False)

    seg_pos = jnp.arange(SEGS, dtype=jnp.float32)
    tail_weight = jnp.exp(-decay_rate[:, None, :] * seg_len * (SEGS - 1.0 - seg_pos)[None, :, None])
    own_state = jnp.sum(tail_weight * seg_end, 1)
    blocks = lax.axis_size("ctx")
    mine = lax.axis_index("ctx")
    ring = 4 if blocks % 4 == 0 else blocks
    place = (mine % ring).astype(jnp.float32)
    span = -decay_rate * seq_rows
    entering = jnp.zeros_like(own_state)
    total = jnp.exp(span * (ring - 1.0 - place)) * own_state
    for step in range(1, ring):
        pairs = [(b0 + z, b0 + (z + step) % ring) for b0 in range(0, blocks, ring) for z in range(ring)]
        arrived = lax.ppermute(own_state, "ctx", pairs)
        source = jnp.where(place >= step, place - step, place - step + ring)
        entering = entering + jnp.where(place >= step, jnp.exp(span * (step - 1.0)), 0.0) * arrived
        total = total + jnp.exp(span * (ring - 1.0 - source)) * arrived
    group = mine // ring
    for back in range(1, blocks // ring):
        moved = from_behind(total, "ctx", ring * back)
        weight = jnp.exp(span * (place + ring * (back - 1.0)))
        entering = entering + jnp.where(group >= back, weight, 0.0) * moved
    seg_gap = seg_pos[:, None] - 1.0 - seg_pos[None, :]
    seg_mix = jnp.where(
        (seg_gap >= 0.0)[:, :, None, None],
        jnp.exp(-decay_rate[None, None] * seg_len * jnp.maximum(seg_gap, 0.0)[:, :, None, None]),
        0.0,
    )
    seg_init = jnp.einsum("jirc,ric->rjc", seg_mix, seg_end, precision=lax.Precision.HIGHEST)
    gated, _ = modal_scan(driven, poles, mode_gain, seg_init, True, query_part, skip_gain)
    carried = mode_gain[:, None, :] * jnp.exp(
        -decay_rate[:, None, :] * seg_len * seg_pos[None, :, None]
    ) * entering[:, None, :]
    gated = add_carried(poles, query_part, gated, carried)
    gated = gated.astype(jnp.bfloat16)
    gated = gated.reshape(sources, chunks, rows, group_chans)
    outs = []
    for q in range(chunks):
        rounded = jnp.einsum(
            "slc,cn->sln", gated[:, q], out_weight, preferred_element_type=jnp.float32
        ).astype(jnp.bfloat16)
        outs.append(lax.psum_scatter(rounded, "chan", scatter_dimension=0, tiled=False))
    return jnp.concatenate(outs, 0)


def solution(mesh):
    return jax.shard_map(
        local,
        mesh=mesh,
        in_specs=(
            P(("ctx", "chan"), None),
            P(None, None, "chan"),
            P(None, None, "chan"),
            P(None, "chan"),
            P(None, "chan"),
            P("chan"),
            P("chan", None),
        ),
        out_specs=P(("ctx", "chan"), None),
        check_vma=False,
    )
```

```python
import functools

import jax
import jax.numpy as jnp
from jax import lax
from jax.experimental import pallas as pl
from jax.sharding import PartitionSpec as P

SEGS = 8
LANES = 128
CHUNKS = 1


def from_behind(array, axis, by):
    size = lax.axis_size(axis)
    pairs = [(i, i + by) for i in range(size) if 0 <= i + by < size]
    return lax.ppermute(array, axis, pairs)


def scan_kernel(x_ref, p_ref, g_ref, *refs, steps, segs, with_y):
    modes = p_ref.shape[0]
    lanes = x_ref.shape[1]
    poles = [jnp.broadcast_to(p_ref[pl.ds(r, 1), :], (segs, lanes)) for r in range(modes)]
    if with_y:
        q_ref, skip_ref, s0_ref, y_ref, end_ref = refs
        skip = jnp.broadcast_to(skip_ref[...], (segs, lanes))
        gains = [jnp.broadcast_to(g_ref[pl.ds(r, 1), :], (segs, lanes)) for r in range(modes)]
        start = tuple(s0_ref[r] for r in range(modes))
    else:
        (end_ref,) = refs
        start = tuple(jnp.zeros((segs, lanes), jnp.float32) for r in range(modes))

    def body(k, state):
        drive = x_ref[pl.ds(k, segs, stride=steps), :]
        state = tuple(poles[r] * state[r] + drive for r in range(modes))
        if with_y:
            acc = gains[0] * state[0]
            for r in range(1, modes):
                acc = acc + gains[r] * state[r]
            rows = pl.ds(k, segs, stride=steps)
            y_ref[rows, :] = q_ref[rows, :] * (acc + skip * drive)
        return state

    state = lax.fori_loop(0, steps, body, start, unroll=8)
    for r in range(modes):
        end_ref[r] = state[r]


def modal_scan(x, poles, gains, init, with_y, query=None, skip=None):
    seq_rows, chans = x.shape
    modes = poles.shape[0]
    steps = seq_rows // SEGS
    state_spec = pl.BlockSpec((modes, SEGS, LANES), lambda i: (0, 0, i))
    param_spec = pl.BlockSpec((modes, LANES), lambda i: (0, i))
    x_spec = pl.BlockSpec((seq_rows, LANES), lambda i: (0, i))
    end_shape = jax.ShapeDtypeStruct((modes, SEGS, chans), jnp.float32)
    in_specs = [x_spec, param_spec, param_spec]
    operands = [x, poles, gains]
    if with_y:
        out_shape = (jax.ShapeDtypeStruct((seq_rows, chans), jnp.float32), end_shape)
        out_specs = (x_spec, state_spec)
        in_specs += [x_spec, pl.BlockSpec((1, LANES), lambda i: (0, i)), state_spec]
        operands += [query, skip.reshape(1, chans), init]
    else:
        out_shape = (end_shape,)
        out_specs = (state_spec,)
    return pl.pallas_call(
        functools.partial(scan_kernel, steps=steps, segs=SEGS, with_y=with_y),
        grid=(chans // LANES,),
        in_specs=in_specs,
        out_specs=out_specs,
        out_shape=out_shape,
    )(*operands)


def local(tokens, in_weight, short_weight, decay_rate, residue, skip_gain, out_weight):
    group_chans = in_weight.shape[2]
    filter_taps = short_weight.shape[0]
    modes = decay_rate.shape[0]
    chunks = CHUNKS
    rows = tokens.shape[0] // chunks
    parts = []
    for q in range(chunks):
        gathered = lax.all_gather(tokens[q * rows : (q + 1) * rows], "chan", axis=0)
        parts.append(
            jnp.einsum("sld,jdc->sljc", gathered, in_weight, preferred_element_type=jnp.float32).astype(
                jnp.bfloat16
            )
        )
    sources = parts[0].shape[0]
    seq_rows = sources * chunks * rows
    projected = jnp.stack(parts, 1).reshape(seq_rows, 3, group_chans)
    tail = projected[seq_rows - (filter_taps - 1) :]
    earlier_rows = from_behind(tail, "ctx", 1)
    padded = jnp.concatenate([earlier_rows, projected], 0)
    features = jnp.zeros((seq_rows, 3, group_chans), jnp.float32)
    for offset in range(filter_taps):
        features = features + short_weight[offset] * padded[
            filter_taps - 1 - offset : filter_taps - 1 - offset + seq_rows
        ].astype(jnp.float32)
    query_part = features[:, 0]
    driven = features[:, 1] * features[:, 2]

    seg_len = seq_rows // SEGS
    poles = jnp.exp(-decay_rate)
    mode_gain = residue * jnp.sqrt(2.0 * decay_rate)
    (seg_end,) = modal_scan(driven, poles, mode_gain, None, False)

    seg_pos = jnp.arange(SEGS, dtype=jnp.float32)
    tail_weight = jnp.exp(-decay_rate[:, None, :] * seg_len * (SEGS - 1.0 - seg_pos)[None, :, None])
    own_state = jnp.sum(tail_weight * seg_end, 1)
    blocks = lax.axis_size("ctx")
    mine = lax.axis_index("ctx")
    ring = 4 if blocks % 4 == 0 else blocks
    place = (mine % ring).astype(jnp.float32)
    span = -decay_rate * seq_rows
    entering = jnp.zeros_like(own_state)
    total = jnp.exp(span * (ring - 1.0 - place)) * own_state
    for step in range(1, ring):
        pairs = [(b0 + z, b0 + (z + step) % ring) for b0 in range(0, blocks, ring) for z in range(ring)]
        arrived = lax.ppermute(own_state, "ctx", pairs)
        source = jnp.where(place >= step, place - step, place - step + ring)
        entering = entering + jnp.where(place >= step, jnp.exp(span * (step - 1.0)), 0.0) * arrived
        total = total + jnp.exp(span * (ring - 1.0 - source)) * arrived
    group = mine // ring
    for back in range(1, blocks // ring):
        moved = from_behind(total, "ctx", ring * back)
        weight = jnp.exp(span * (place + ring * (back - 1.0)))
        entering = entering + jnp.where(group >= back, weight, 0.0) * moved
    seg_gap = seg_pos[:, None] - 1.0 - seg_pos[None, :]
    seg_mix = jnp.where(
        (seg_gap >= 0.0)[:, :, None, None],
        jnp.exp(-decay_rate[None, None] * seg_len * jnp.maximum(seg_gap, 0.0)[:, :, None, None]),
        0.0,
    )
    seg_init = jnp.einsum("jirc,ric->rjc", seg_mix, seg_end, precision=lax.Precision.HIGHEST)
    seg_init = seg_init + jnp.exp(
        -decay_rate[:, None, :] * seg_len * seg_pos[None, :, None]
    ) * entering[:, None, :]
    gated, _ = modal_scan(driven, poles, mode_gain, seg_init, True, query_part, skip_gain)
    gated = gated.astype(jnp.bfloat16)
    gated = gated.reshape(sources, chunks, rows, group_chans)
    outs = []
    for q in range(chunks):
        rounded = jnp.einsum(
            "slc,cn->sln", gated[:, q], out_weight, preferred_element_type=jnp.float32
        ).astype(jnp.bfloat16)
        outs.append(lax.psum_scatter(rounded, "chan", scatter_dimension=0, tiled=False))
    return jnp.concatenate(outs, 0)


def solution(mesh):
    return jax.shard_map(
        local,
        mesh=mesh,
        in_specs=(
            P(("ctx", "chan"), None),
            P(None, None, "chan"),
            P(None, None, "chan"),
            P(None, "chan"),
            P(None, "chan"),
            P("chan"),
            P("chan", None),
        ),
        out_specs=P(("ctx", "chan"), None),
        check_vma=False,
    )
```

```python
import functools

import jax
import jax.numpy as jnp
from jax import lax
from jax.experimental import pallas as pl
from jax.sharding import PartitionSpec as P

SEGS = 8
LANES = 128
CHUNKS = 1


def from_behind(array, axis, by):
    size = lax.axis_size(axis)
    pairs = [(i, i + by) for i in range(size) if 0 <= i + by < size]
    return lax.ppermute(array, axis, pairs)


def scan_kernel(x_ref, p_ref, g_ref, *refs, steps, segs, with_y):
    modes = p_ref.shape[0]
    lanes = x_ref.shape[1]
    poles = [jnp.broadcast_to(p_ref[pl.ds(r, 1), :], (segs, lanes)) for r in range(modes)]
    if with_y:
        q_ref, skip_ref, s0_ref, y_ref, end_ref = refs
        skip = jnp.broadcast_to(skip_ref[...], (segs, lanes))
        gains = [jnp.broadcast_to(g_ref[pl.ds(r, 1), :], (segs, lanes)) for r in range(modes)]
        start = tuple(s0_ref[r] for r in range(modes))
    else:
        (end_ref,) = refs
        start = tuple(jnp.zeros((segs, lanes), jnp.float32) for r in range(modes))

    def body(k, state):
        drive = x_ref[pl.ds(k, segs, stride=steps), :]
        state = tuple(poles[r] * state[r] + drive for r in range(modes))
        if with_y:
            acc = gains[0] * state[0]
            for r in range(1, modes):
                acc = acc + gains[r] * state[r]
            rows = pl.ds(k, segs, stride=steps)
            y_ref[rows, :] = q_ref[rows, :] * (acc + skip * drive)
        return state

    state = lax.fori_loop(0, steps, body, start, unroll=8)
    for r in range(modes):
        end_ref[r] = state[r]


def modal_scan(x, poles, gains, init, with_y, query=None, skip=None):
    seq_rows, chans = x.shape
    modes = poles.shape[0]
    steps = seq_rows // SEGS
    state_spec = pl.BlockSpec((modes, SEGS, LANES), lambda i: (0, 0, i))
    param_spec = pl.BlockSpec((modes, LANES), lambda i: (0, i))
    x_spec = pl.BlockSpec((seq_rows, LANES), lambda i: (0, i))
    end_shape = jax.ShapeDtypeStruct((modes, SEGS, chans), jnp.float32)
    in_specs = [x_spec, param_spec, param_spec]
    operands = [x, poles, gains]
    if with_y:
        out_shape = (jax.ShapeDtypeStruct((seq_rows, chans), jnp.float32), end_shape)
        out_specs = (x_spec, state_spec)
        in_specs += [x_spec, pl.BlockSpec((1, LANES), lambda i: (0, i)), state_spec]
        operands += [query, skip.reshape(1, chans), init]
    else:
        out_shape = (end_shape,)
        out_specs = (state_spec,)
    return pl.pallas_call(
        functools.partial(scan_kernel, steps=steps, segs=SEGS, with_y=with_y),
        grid=(chans // LANES,),
        in_specs=in_specs,
        out_specs=out_specs,
        out_shape=out_shape,
    )(*operands)


def local(tokens, in_weight, short_weight, decay_rate, residue, skip_gain, out_weight):
    group_chans = in_weight.shape[2]
    filter_taps = short_weight.shape[0]
    modes = decay_rate.shape[0]
    chunks = CHUNKS
    rows = tokens.shape[0] // chunks
    parts = []
    for q in range(chunks):
        gathered = lax.all_gather(tokens[q * rows : (q + 1) * rows], "chan", axis=0)
        parts.append(
            jnp.einsum("sld,jdc->sljc", gathered, in_weight, preferred_element_type=jnp.float32).astype(
                jnp.bfloat16
            )
        )
    sources = parts[0].shape[0]
    seq_rows = sources * chunks * rows
    projected = jnp.stack(parts, 1).reshape(seq_rows, 3, group_chans)
    tail = projected[seq_rows - (filter_taps - 1) :]
    earlier_rows = from_behind(tail, "ctx", 1)
    padded = jnp.concatenate([earlier_rows, projected], 0)
    features = jnp.zeros((seq_rows, 3, group_chans), jnp.float32)
    for offset in range(filter_taps):
        features = features + short_weight[offset] * padded[
            filter_taps - 1 - offset : filter_taps - 1 - offset + seq_rows
        ].astype(jnp.float32)
    query_part = features[:, 0]
    driven = features[:, 1] * features[:, 2]

    seg_len = seq_rows // SEGS
    poles = jnp.exp(-decay_rate)
    mode_gain = residue * jnp.sqrt(2.0 * decay_rate)
    (seg_end,) = modal_scan(driven, poles, mode_gain, None, False)

    seg_pos = jnp.arange(SEGS, dtype=jnp.float32)
    tail_weight = jnp.exp(-decay_rate[:, None, :] * seg_len * (SEGS - 1.0 - seg_pos)[None, :, None])
    own_state = jnp.sum(tail_weight * seg_end, 1)
    blocks = lax.axis_size("ctx")
    mine = lax.axis_index("ctx")
    states = lax.all_to_all(jnp.broadcast_to(own_state[None], (blocks,) + own_state.shape), "ctx", 0, 0)
    back = (mine - 1 - jnp.arange(blocks)).astype(jnp.float32)
    block_weight = jnp.where(
        (back >= 0.0)[:, None, None],
        jnp.exp(-decay_rate[None] * seq_rows * jnp.maximum(back, 0.0)[:, None, None]),
        0.0,
    )
    entering = jnp.sum(block_weight * states, 0)
    seg_gap = seg_pos[:, None] - 1.0 - seg_pos[None, :]
    seg_mix = jnp.where(
        (seg_gap >= 0.0)[:, :, None, None],
        jnp.exp(-decay_rate[None, None] * seg_len * jnp.maximum(seg_gap, 0.0)[:, :, None, None]),
        0.0,
    )
    seg_init = jnp.einsum("jirc,ric->rjc", seg_mix, seg_end, precision=lax.Precision.HIGHEST)
    seg_init = seg_init + jnp.exp(
        -decay_rate[:, None, :] * seg_len * seg_pos[None, :, None]
    ) * entering[:, None, :]
    gated, _ = modal_scan(driven, poles, mode_gain, seg_init, True, query_part, skip_gain)
    gated = gated.astype(jnp.bfloat16)
    gated = gated.reshape(sources, chunks, rows, group_chans)
    outs = []
    for q in range(chunks):
        rounded = jnp.einsum(
            "slc,cn->sln", gated[:, q], out_weight, preferred_element_type=jnp.float32
        ).astype(jnp.bfloat16)
        outs.append(lax.psum_scatter(rounded, "chan", scatter_dimension=0, tiled=False))
    return jnp.concatenate(outs, 0)


def solution(mesh):
    return jax.shard_map(
        local,
        mesh=mesh,
        in_specs=(
            P(("ctx", "chan"), None),
            P(None, None, "chan"),
            P(None, None, "chan"),
            P(None, "chan"),
            P(None, "chan"),
            P("chan"),
            P("chan", None),
        ),
        out_specs=P(("ctx", "chan"), None),
        check_vma=False,
    )
```

```python
import functools

import jax
import jax.numpy as jnp
from jax import lax
from jax.experimental import pallas as pl
from jax.experimental.pallas import tpu as pltpu
from jax.sharding import PartitionSpec as P

SEGS = 8
LANES = 128
CHUNKS = 1


def from_behind(array, axis, by):
    size = lax.axis_size(axis)
    pairs = [(i, i + by) for i in range(size) if 0 <= i + by < size]
    return lax.ppermute(array, axis, pairs)


def scan_kernel(x_ref, p_ref, g_ref, *refs, steps, segs, with_y):
    if with_y:
        refs, staged = refs[:-1], refs[-1]
    modes = p_ref.shape[0]
    lanes = x_ref.shape[1]
    poles = [jnp.broadcast_to(p_ref[pl.ds(r, 1), :], (segs, lanes)) for r in range(modes)]
    if with_y:
        q_ref, skip_ref, s0_ref, y_ref, end_ref = refs
        skip = jnp.broadcast_to(skip_ref[...], (segs, lanes))
        gains = [jnp.broadcast_to(g_ref[pl.ds(r, 1), :], (segs, lanes)) for r in range(modes)]
        start = tuple(s0_ref[r] for r in range(modes))
    else:
        (end_ref,) = refs
        start = tuple(jnp.zeros((segs, lanes), jnp.float32) for r in range(modes))

    def body(k, state):
        drive = x_ref[pl.ds(k, segs, stride=steps), :]
        state = tuple(poles[r] * state[r] + drive for r in range(modes))
        if with_y:
            acc = gains[0] * state[0]
            for r in range(1, modes):
                acc = acc + gains[r] * state[r]
            rows = pl.ds(k, segs, stride=steps)
            staged[rows, :] = q_ref[rows, :] * (acc + skip * drive)
        return state

    state = lax.fori_loop(0, steps, body, start, unroll=8)
    for r in range(modes):
        end_ref[r] = state[r]
    if with_y:
        y_ref[...] = staged[...].astype(y_ref.dtype)


def modal_scan(x, poles, gains, init, with_y, query=None, skip=None):
    seq_rows, chans = x.shape
    modes = poles.shape[0]
    steps = seq_rows // SEGS
    state_spec = pl.BlockSpec((modes, SEGS, LANES), lambda i: (0, 0, i))
    param_spec = pl.BlockSpec((modes, LANES), lambda i: (0, i))
    x_spec = pl.BlockSpec((seq_rows, LANES), lambda i: (0, i))
    end_shape = jax.ShapeDtypeStruct((modes, SEGS, chans), jnp.float32)
    in_specs = [x_spec, param_spec, param_spec]
    operands = [x, poles, gains]
    if with_y:
        out_shape = (jax.ShapeDtypeStruct((seq_rows, chans), jnp.bfloat16), end_shape)
        out_specs = (x_spec, state_spec)
        in_specs += [x_spec, pl.BlockSpec((1, LANES), lambda i: (0, i)), state_spec]
        operands += [query, skip.reshape(1, chans), init]
    else:
        out_shape = (end_shape,)
        out_specs = (state_spec,)
    scratch = [pltpu.VMEM((seq_rows, LANES), jnp.float32)] if with_y else []
    return pl.pallas_call(
        functools.partial(scan_kernel, steps=steps, segs=SEGS, with_y=with_y),
        grid=(chans // LANES,),
        scratch_shapes=scratch,
        in_specs=in_specs,
        out_specs=out_specs,
        out_shape=out_shape,
    )(*operands)


def local(tokens, in_weight, short_weight, decay_rate, residue, skip_gain, out_weight):
    group_chans = in_weight.shape[2]
    filter_taps = short_weight.shape[0]
    modes = decay_rate.shape[0]
    chunks = CHUNKS
    rows = tokens.shape[0] // chunks
    parts = []
    for q in range(chunks):
        gathered = lax.all_gather(tokens[q * rows : (q + 1) * rows], "chan", axis=0)
        parts.append(
            jnp.einsum("sld,jdc->sljc", gathered, in_weight, preferred_element_type=jnp.float32).astype(
                jnp.bfloat16
            )
        )
    sources = parts[0].shape[0]
    seq_rows = sources * chunks * rows
    projected = jnp.stack(parts, 1).reshape(seq_rows, 3, group_chans)
    tail = projected[seq_rows - (filter_taps - 1) :]
    earlier_rows = from_behind(tail, "ctx", 1)
    padded = jnp.concatenate([earlier_rows, projected], 0)
    features = jnp.zeros((seq_rows, 3, group_chans), jnp.float32)
    for offset in range(filter_taps):
        features = features + short_weight[offset] * padded[
            filter_taps - 1 - offset : filter_taps - 1 - offset + seq_rows
        ].astype(jnp.float32)
    query_part = features[:, 0]
    driven = features[:, 1] * features[:, 2]

    seg_len = seq_rows // SEGS
    poles = jnp.exp(-decay_rate)
    mode_gain = residue * jnp.sqrt(2.0 * decay_rate)
    (seg_end,) = modal_scan(driven, poles, mode_gain, None, False)

    seg_pos = jnp.arange(SEGS, dtype=jnp.float32)
    tail_weight = jnp.exp(-decay_rate[:, None, :] * seg_len * (SEGS - 1.0 - seg_pos)[None, :, None])
    own_state = jnp.sum(tail_weight * seg_end, 1)
    blocks = lax.axis_size("ctx")
    mine = lax.axis_index("ctx")
    states = lax.all_to_all(jnp.broadcast_to(own_state[None], (blocks,) + own_state.shape), "ctx", 0, 0)
    back = (mine - 1 - jnp.arange(blocks)).astype(jnp.float32)
    block_weight = jnp.where(
        (back >= 0.0)[:, None, None],
        jnp.exp(-decay_rate[None] * seq_rows * jnp.maximum(back, 0.0)[:, None, None]),
        0.0,
    )
    entering = jnp.sum(block_weight * states, 0)
    seg_gap = seg_pos[:, None] - 1.0 - seg_pos[None, :]
    seg_mix = jnp.where(
        (seg_gap >= 0.0)[:, :, None, None],
        jnp.exp(-decay_rate[None, None] * seg_len * jnp.maximum(seg_gap, 0.0)[:, :, None, None]),
        0.0,
    )
    seg_init = jnp.einsum("jirc,ric->rjc", seg_mix, seg_end, precision=lax.Precision.HIGHEST)
    seg_init = seg_init + jnp.exp(
        -decay_rate[:, None, :] * seg_len * seg_pos[None, :, None]
    ) * entering[:, None, :]
    gated, _ = modal_scan(driven, poles, mode_gain, seg_init, True, query_part, skip_gain)
    gated = gated.reshape(sources, chunks, rows, group_chans)
    outs = []
    for q in range(chunks):
        rounded = jnp.einsum(
            "slc,cn->sln", gated[:, q], out_weight, preferred_element_type=jnp.float32
        ).astype(jnp.bfloat16)
        outs.append(lax.psum_scatter(rounded, "chan", scatter_dimension=0, tiled=False))
    return jnp.concatenate(outs, 0)


def solution(mesh):
    return jax.shard_map(
        local,
        mesh=mesh,
        in_specs=(
            P(("ctx", "chan"), None),
            P(None, None, "chan"),
            P(None, None, "chan"),
            P(None, "chan"),
            P(None, "chan"),
            P("chan"),
            P("chan", None),
        ),
        out_specs=P(("ctx", "chan"), None),
        check_vma=False,
    )
```

```python
import functools

import jax
import jax.numpy as jnp
from jax import lax
from jax.experimental import pallas as pl
from jax.experimental.pallas import tpu as pltpu
from jax.sharding import PartitionSpec as P

SEGS = 8
LANES = 128
CHUNKS = 1


def from_behind(array, axis, by):
    size = lax.axis_size(axis)
    pairs = [(i, i + by) for i in range(size) if 0 <= i + by < size]
    return lax.ppermute(array, axis, pairs)


def scan_kernel(x_ref, p_ref, g_ref, *refs, steps, segs, with_y):
    if with_y:
        refs, staged = refs[:-1], refs[-1]
    modes = p_ref.shape[0]
    lanes = x_ref.shape[1]
    poles = [jnp.broadcast_to(p_ref[pl.ds(r, 1), :], (segs, lanes)) for r in range(modes)]
    if with_y:
        q_ref, skip_ref, s0_ref, y_ref, end_ref = refs
        skip = jnp.broadcast_to(skip_ref[...], (segs, lanes))
        gains = [jnp.broadcast_to(g_ref[pl.ds(r, 1), :], (segs, lanes)) for r in range(modes)]
        start = tuple(s0_ref[r] for r in range(modes))
    else:
        (end_ref,) = refs
        start = tuple(jnp.zeros((segs, lanes), jnp.float32) for r in range(modes))

    def body(k, state):
        drive = x_ref[pl.ds(k, segs, stride=steps), :]
        state = tuple(poles[r] * state[r] + drive for r in range(modes))
        if with_y:
            acc = gains[0] * state[0]
            for r in range(1, modes):
                acc = acc + gains[r] * state[r]
            rows = pl.ds(k, segs, stride=steps)
            staged[rows, :] = q_ref[rows, :] * (acc + skip * drive)
        return state

    state = lax.fori_loop(0, steps, body, start, unroll=8)
    for r in range(modes):
        end_ref[r] = state[r]
    if with_y:
        y_ref[...] = staged[...].astype(y_ref.dtype)


def modal_scan(x, poles, gains, init, with_y, query=None, skip=None):
    seq_rows, chans = x.shape
    modes = poles.shape[0]
    steps = seq_rows // SEGS
    state_spec = pl.BlockSpec((modes, SEGS, LANES), lambda i: (0, 0, i))
    param_spec = pl.BlockSpec((modes, LANES), lambda i: (0, i))
    x_spec = pl.BlockSpec((seq_rows, LANES), lambda i: (0, i))
    end_shape = jax.ShapeDtypeStruct((modes, SEGS, chans), jnp.float32)
    in_specs = [x_spec, param_spec, param_spec]
    operands = [x, poles, gains]
    if with_y:
        out_shape = (jax.ShapeDtypeStruct((seq_rows, chans), jnp.bfloat16), end_shape)
        out_specs = (x_spec, state_spec)
        in_specs += [x_spec, pl.BlockSpec((1, LANES), lambda i: (0, i)), state_spec]
        operands += [query, skip.reshape(1, chans), init]
    else:
        out_shape = (end_shape,)
        out_specs = (state_spec,)
    scratch = [pltpu.VMEM((seq_rows, LANES), jnp.float32)] if with_y else []
    return pl.pallas_call(
        functools.partial(scan_kernel, steps=steps, segs=SEGS, with_y=with_y),
        grid=(chans // LANES,),
        scratch_shapes=scratch,
        in_specs=in_specs,
        out_specs=out_specs,
        out_shape=out_shape,
    )(*operands)


def local(tokens, in_weight, short_weight, decay_rate, residue, skip_gain, out_weight):
    group_chans = in_weight.shape[2]
    filter_taps = short_weight.shape[0]
    modes = decay_rate.shape[0]
    chunks = CHUNKS
    rows = tokens.shape[0] // chunks
    weight_cols = in_weight.transpose(1, 0, 2).reshape(in_weight.shape[1], 3 * group_chans)
    parts = []
    for q in range(chunks):
        gathered = lax.all_gather(tokens[q * rows : (q + 1) * rows], "chan", axis=0)
        flat = lax.dot_general(
            gathered.reshape(-1, gathered.shape[-1]), weight_cols, (((1,), (0,)), ((), ())),
            preferred_element_type=jnp.float32,
        ).astype(jnp.bfloat16)
        parts.append(flat.reshape(gathered.shape[0], rows, 3, group_chans))
    sources = parts[0].shape[0]
    seq_rows = sources * chunks * rows
    projected = jnp.stack(parts, 1).reshape(seq_rows, 3, group_chans)
    tail = projected[seq_rows - (filter_taps - 1) :]
    earlier_rows = from_behind(tail, "ctx", 1)
    padded = jnp.concatenate([earlier_rows, projected], 0)
    features = jnp.zeros((seq_rows, 3, group_chans), jnp.float32)
    for offset in range(filter_taps):
        features = features + short_weight[offset] * padded[
            filter_taps - 1 - offset : filter_taps - 1 - offset + seq_rows
        ].astype(jnp.float32)
    query_part = features[:, 0]
    driven = features[:, 1] * features[:, 2]

    seg_len = seq_rows // SEGS
    poles = jnp.exp(-decay_rate)
    mode_gain = residue * jnp.sqrt(2.0 * decay_rate)
    (seg_end,) = modal_scan(driven, poles, mode_gain, None, False)

    seg_pos = jnp.arange(SEGS, dtype=jnp.float32)
    tail_weight = jnp.exp(-decay_rate[:, None, :] * seg_len * (SEGS - 1.0 - seg_pos)[None, :, None])
    own_state = jnp.sum(tail_weight * seg_end, 1)
    blocks = lax.axis_size("ctx")
    mine = lax.axis_index("ctx")
    states = lax.all_to_all(jnp.broadcast_to(own_state[None], (blocks,) + own_state.shape), "ctx", 0, 0)
    back = (mine - 1 - jnp.arange(blocks)).astype(jnp.float32)
    block_weight = jnp.where(
        (back >= 0.0)[:, None, None],
        jnp.exp(-decay_rate[None] * seq_rows * jnp.maximum(back, 0.0)[:, None, None]),
        0.0,
    )
    entering = jnp.sum(block_weight * states, 0)
    seg_gap = seg_pos[:, None] - 1.0 - seg_pos[None, :]
    seg_mix = jnp.where(
        (seg_gap >= 0.0)[:, :, None, None],
        jnp.exp(-decay_rate[None, None] * seg_len * jnp.maximum(seg_gap, 0.0)[:, :, None, None]),
        0.0,
    )
    seg_init = jnp.einsum("jirc,ric->rjc", seg_mix, seg_end, precision=lax.Precision.HIGHEST)
    seg_init = seg_init + jnp.exp(
        -decay_rate[:, None, :] * seg_len * seg_pos[None, :, None]
    ) * entering[:, None, :]
    gated, _ = modal_scan(driven, poles, mode_gain, seg_init, True, query_part, skip_gain)
    gated = gated.reshape(sources, chunks, rows, group_chans)
    outs = []
    for q in range(chunks):
        rounded = jnp.einsum(
            "slc,cn->sln", gated[:, q], out_weight, preferred_element_type=jnp.float32
        ).astype(jnp.bfloat16)
        outs.append(lax.psum_scatter(rounded, "chan", scatter_dimension=0, tiled=False))
    return jnp.concatenate(outs, 0)


def solution(mesh):
    return jax.shard_map(
        local,
        mesh=mesh,
        in_specs=(
            P(("ctx", "chan"), None),
            P(None, None, "chan"),
            P(None, None, "chan"),
            P(None, "chan"),
            P(None, "chan"),
            P("chan"),
            P("chan", None),
        ),
        out_specs=P(("ctx", "chan"), None),
        check_vma=False,
    )
```

```python
import functools

import jax
import jax.numpy as jnp
from jax import lax
from jax.experimental import pallas as pl
from jax.experimental.pallas import tpu as pltpu
from jax.sharding import PartitionSpec as P

SEGS = 8
LANES = 128
CHUNKS = 1


def from_behind(array, axis, by):
    size = lax.axis_size(axis)
    pairs = [(i, i + by) for i in range(size) if 0 <= i + by < size]
    return lax.ppermute(array, axis, pairs)


def scan_kernel(x_ref, p_ref, g_ref, *refs, steps, segs, with_y):
    if with_y:
        refs, staged = refs[:-1], refs[-1]
    modes = p_ref.shape[0]
    lanes = x_ref.shape[1]
    poles = [jnp.broadcast_to(p_ref[pl.ds(r, 1), :], (segs, lanes)) for r in range(modes)]
    if with_y:
        q_ref, skip_ref, s0_ref, y_ref, end_ref = refs
        skip = jnp.broadcast_to(skip_ref[...], (segs, lanes))
        gains = [jnp.broadcast_to(g_ref[pl.ds(r, 1), :], (segs, lanes)) for r in range(modes)]
        start = tuple(s0_ref[r] for r in range(modes))
    else:
        (end_ref,) = refs
        start = tuple(jnp.zeros((segs, lanes), jnp.float32) for r in range(modes))

    def body(k, state):
        drive = x_ref[pl.ds(k, segs, stride=steps), :]
        state = tuple(poles[r] * state[r] + drive for r in range(modes))
        if with_y:
            acc = gains[0] * state[0]
            for r in range(1, modes):
                acc = acc + gains[r] * state[r]
            rows = pl.ds(k, segs, stride=steps)
            staged[rows, :] = q_ref[rows, :] * (acc + skip * drive)
        return state

    state = lax.fori_loop(0, steps, body, start, unroll=8)
    for r in range(modes):
        end_ref[r] = state[r]
    if with_y:
        y_ref[...] = staged[...].astype(y_ref.dtype)


def modal_scan(x, poles, gains, init, with_y, query=None, skip=None):
    seq_rows, chans = x.shape
    modes = poles.shape[0]
    steps = seq_rows // SEGS
    state_spec = pl.BlockSpec((modes, SEGS, LANES), lambda i: (0, 0, i))
    param_spec = pl.BlockSpec((modes, LANES), lambda i: (0, i))
    x_spec = pl.BlockSpec((seq_rows, LANES), lambda i: (0, i))
    end_shape = jax.ShapeDtypeStruct((modes, SEGS, chans), jnp.float32)
    in_specs = [x_spec, param_spec, param_spec]
    operands = [x, poles, gains]
    if with_y:
        out_shape = (jax.ShapeDtypeStruct((seq_rows, chans), jnp.bfloat16), end_shape)
        out_specs = (x_spec, state_spec)
        in_specs += [x_spec, pl.BlockSpec((1, LANES), lambda i: (0, i)), state_spec]
        operands += [query, skip.reshape(1, chans), init]
    else:
        out_shape = (end_shape,)
        out_specs = (state_spec,)
    scratch = [pltpu.VMEM((seq_rows, LANES), jnp.float32)] if with_y else []
    return pl.pallas_call(
        functools.partial(scan_kernel, steps=steps, segs=SEGS, with_y=with_y),
        grid=(chans // LANES,),
        scratch_shapes=scratch,
        in_specs=in_specs,
        out_specs=out_specs,
        out_shape=out_shape,
    )(*operands)


def local(tokens, in_weight, short_weight, decay_rate, residue, skip_gain, out_weight):
    group_chans = in_weight.shape[2]
    filter_taps = short_weight.shape[0]
    modes = decay_rate.shape[0]
    chunks = CHUNKS
    rows = tokens.shape[0] // chunks
    parts = []
    for q in range(chunks):
        gathered = lax.all_gather(tokens[q * rows : (q + 1) * rows], "chan", axis=0)
        parts.append(
            jnp.einsum("sld,jdc->sljc", gathered, in_weight, preferred_element_type=jnp.float32).astype(
                jnp.bfloat16
            )
        )
    sources = parts[0].shape[0]
    seq_rows = sources * chunks * rows
    projected = jnp.stack(parts, 1).reshape(seq_rows, 3, group_chans)
    tail = projected[seq_rows - (filter_taps - 1) :]
    earlier_rows = from_behind(tail, "ctx", 1)
    padded = jnp.concatenate([earlier_rows, projected], 0)

    def feature(kind):
        total = short_weight[0, kind] * padded[filter_taps - 1 :, kind].astype(jnp.float32)
        for offset in range(1, filter_taps):
            total = total + short_weight[offset, kind] * padded[
                filter_taps - 1 - offset : filter_taps - 1 - offset + seq_rows, kind
            ].astype(jnp.float32)
        return total

    query_part = feature(0)
    driven = feature(1) * feature(2)

    seg_len = seq_rows // SEGS
    poles = jnp.exp(-decay_rate)
    mode_gain = residue * jnp.sqrt(2.0 * decay_rate)
    (seg_end,) = modal_scan(driven, poles, mode_gain, None, False)

    seg_pos = jnp.arange(SEGS, dtype=jnp.float32)
    tail_weight = jnp.exp(-decay_rate[:, None, :] * seg_len * (SEGS - 1.0 - seg_pos)[None, :, None])
    own_state = jnp.sum(tail_weight * seg_end, 1)
    blocks = lax.axis_size("ctx")
    mine = lax.axis_index("ctx")
    states = lax.all_to_all(jnp.broadcast_to(own_state[None], (blocks,) + own_state.shape), "ctx", 0, 0)
    back = (mine - 1 - jnp.arange(blocks)).astype(jnp.float32)
    block_weight = jnp.where(
        (back >= 0.0)[:, None, None],
        jnp.exp(-decay_rate[None] * seq_rows * jnp.maximum(back, 0.0)[:, None, None]),
        0.0,
    )
    entering = jnp.sum(block_weight * states, 0)
    seg_gap = seg_pos[:, None] - 1.0 - seg_pos[None, :]
    seg_mix = jnp.where(
        (seg_gap >= 0.0)[:, :, None, None],
        jnp.exp(-decay_rate[None, None] * seg_len * jnp.maximum(seg_gap, 0.0)[:, :, None, None]),
        0.0,
    )
    seg_init = jnp.einsum("jirc,ric->rjc", seg_mix, seg_end, precision=lax.Precision.HIGHEST)
    seg_init = seg_init + jnp.exp(
        -decay_rate[:, None, :] * seg_len * seg_pos[None, :, None]
    ) * entering[:, None, :]
    gated, _ = modal_scan(driven, poles, mode_gain, seg_init, True, query_part, skip_gain)
    gated = gated.reshape(sources, chunks, rows, group_chans)
    outs = []
    for q in range(chunks):
        rounded = jnp.einsum(
            "slc,cn->sln", gated[:, q], out_weight, preferred_element_type=jnp.float32
        ).astype(jnp.bfloat16)
        outs.append(lax.psum_scatter(rounded, "chan", scatter_dimension=0, tiled=False))
    return jnp.concatenate(outs, 0)


def solution(mesh):
    return jax.shard_map(
        local,
        mesh=mesh,
        in_specs=(
            P(("ctx", "chan"), None),
            P(None, None, "chan"),
            P(None, None, "chan"),
            P(None, "chan"),
            P(None, "chan"),
            P("chan"),
            P("chan", None),
        ),
        out_specs=P(("ctx", "chan"), None),
        check_vma=False,
    )
```

```python
import functools

import jax
import jax.numpy as jnp
from jax import lax
from jax.experimental import pallas as pl
from jax.experimental.pallas import tpu as pltpu
from jax.sharding import PartitionSpec as P

SEGS = 8
LANES = 128
CHUNKS = 1


def from_behind(array, axis, by):
    size = lax.axis_size(axis)
    pairs = [(i, i + by) for i in range(size) if 0 <= i + by < size]
    return lax.ppermute(array, axis, pairs)


def scan_kernel(x_ref, p_ref, g_ref, *refs, steps, segs, with_y):
    if with_y:
        refs, staged = refs[:-1], refs[-1]
    modes = p_ref.shape[0]
    lanes = x_ref.shape[1]
    poles = [jnp.broadcast_to(p_ref[pl.ds(r, 1), :], (segs, lanes)) for r in range(modes)]
    if with_y:
        q_ref, skip_ref, s0_ref, y_ref, end_ref = refs
        skip = jnp.broadcast_to(skip_ref[...], (segs, lanes))
        gains = [jnp.broadcast_to(g_ref[pl.ds(r, 1), :], (segs, lanes)) for r in range(modes)]
        start = tuple(s0_ref[r] for r in range(modes))
    else:
        (end_ref,) = refs
        start = tuple(jnp.zeros((segs, lanes), jnp.float32) for r in range(modes))

    def body(k, state):
        drive = x_ref[pl.ds(k, segs, stride=steps), :]
        state = tuple(poles[r] * state[r] + drive for r in range(modes))
        if with_y:
            acc = gains[0] * state[0]
            for r in range(1, modes):
                acc = acc + gains[r] * state[r]
            rows = pl.ds(k, segs, stride=steps)
            staged[rows, :] = q_ref[rows, :] * (acc + skip * drive)
        return state

    state = lax.fori_loop(0, steps, body, start, unroll=8)
    for r in range(modes):
        end_ref[r] = state[r]
    if with_y:
        y_ref[...] = staged[...].astype(y_ref.dtype)


def modal_scan(x, poles, gains, init, with_y, query=None, skip=None):
    seq_rows, chans = x.shape
    modes = poles.shape[0]
    steps = seq_rows // SEGS
    state_spec = pl.BlockSpec((modes, SEGS, LANES), lambda i: (0, 0, i))
    param_spec = pl.BlockSpec((modes, LANES), lambda i: (0, i))
    x_spec = pl.BlockSpec((seq_rows, LANES), lambda i: (0, i))
    end_shape = jax.ShapeDtypeStruct((modes, SEGS, chans), jnp.float32)
    in_specs = [x_spec, param_spec, param_spec]
    operands = [x, poles, gains]
    if with_y:
        out_shape = (jax.ShapeDtypeStruct((seq_rows, chans), jnp.bfloat16), end_shape)
        out_specs = (x_spec, state_spec)
        in_specs += [x_spec, pl.BlockSpec((1, LANES), lambda i: (0, i)), state_spec]
        operands += [query, skip.reshape(1, chans), init]
    else:
        out_shape = (end_shape,)
        out_specs = (state_spec,)
    scratch = [pltpu.VMEM((seq_rows, LANES), jnp.float32)] if with_y else []
    return pl.pallas_call(
        functools.partial(scan_kernel, steps=steps, segs=SEGS, with_y=with_y),
        grid=(chans // LANES,),
        scratch_shapes=scratch,
        in_specs=in_specs,
        out_specs=out_specs,
        out_shape=out_shape,
    )(*operands)


def local(tokens, in_weight, short_weight, decay_rate, residue, skip_gain, out_weight):
    group_chans = in_weight.shape[2]
    filter_taps = short_weight.shape[0]
    modes = decay_rate.shape[0]
    width = lax.axis_size("chan")
    tail = tokens[tokens.shape[0] - (filter_taps - 1) :]
    earlier_tokens = jnp.zeros_like(tail)
    for target in range(width):
        pairs = [
            ((block - 1) * width + width - 1, block * width + target)
            for block in range(1, lax.axis_size("ctx"))
        ]
        earlier_tokens = earlier_tokens + lax.ppermute(tail, ("ctx", "chan"), pairs)
    chunks = CHUNKS
    rows = tokens.shape[0] // chunks
    parts = []
    for q in range(chunks):
        gathered = lax.all_gather(tokens[q * rows : (q + 1) * rows], "chan", axis=0)
        parts.append(
            jnp.einsum("sld,jdc->sljc", gathered, in_weight, preferred_element_type=jnp.float32).astype(
                jnp.bfloat16
            )
        )
    sources = parts[0].shape[0]
    seq_rows = sources * chunks * rows
    projected = jnp.stack(parts, 1).reshape(seq_rows, 3, group_chans)
    earlier_rows = jnp.einsum(
        "ld,jdc->ljc", earlier_tokens, in_weight, preferred_element_type=jnp.float32
    ).astype(jnp.bfloat16)
    padded = jnp.concatenate([earlier_rows, projected], 0)

    def feature(kind):
        total = short_weight[0, kind] * padded[filter_taps - 1 :, kind].astype(jnp.float32)
        for offset in range(1, filter_taps):
            total = total + short_weight[offset, kind] * padded[
                filter_taps - 1 - offset : filter_taps - 1 - offset + seq_rows, kind
            ].astype(jnp.float32)
        return total

    query_part = feature(0)
    driven = feature(1) * feature(2)

    seg_len = seq_rows // SEGS
    poles = jnp.exp(-decay_rate)
    mode_gain = residue * jnp.sqrt(2.0 * decay_rate)
    (seg_end,) = modal_scan(driven, poles, mode_gain, None, False)

    seg_pos = jnp.arange(SEGS, dtype=jnp.float32)
    tail_weight = jnp.exp(-decay_rate[:, None, :] * seg_len * (SEGS - 1.0 - seg_pos)[None, :, None])
    own_state = jnp.sum(tail_weight * seg_end, 1)
    blocks = lax.axis_size("ctx")
    mine = lax.axis_index("ctx")
    states = lax.all_to_all(jnp.broadcast_to(own_state[None], (blocks,) + own_state.shape), "ctx", 0, 0)
    back = (mine - 1 - jnp.arange(blocks)).astype(jnp.float32)
    block_weight = jnp.where(
        (back >= 0.0)[:, None, None],
        jnp.exp(-decay_rate[None] * seq_rows * jnp.maximum(back, 0.0)[:, None, None]),
        0.0,
    )
    entering = jnp.sum(block_weight * states, 0)
    seg_gap = seg_pos[:, None] - 1.0 - seg_pos[None, :]
    seg_mix = jnp.where(
        (seg_gap >= 0.0)[:, :, None, None],
        jnp.exp(-decay_rate[None, None] * seg_len * jnp.maximum(seg_gap, 0.0)[:, :, None, None]),
        0.0,
    )
    seg_init = jnp.einsum("jirc,ric->rjc", seg_mix, seg_end, precision=lax.Precision.HIGHEST)
    seg_init = seg_init + jnp.exp(
        -decay_rate[:, None, :] * seg_len * seg_pos[None, :, None]
    ) * entering[:, None, :]
    gated, _ = modal_scan(driven, poles, mode_gain, seg_init, True, query_part, skip_gain)
    gated = gated.reshape(sources, chunks, rows, group_chans)
    outs = []
    for q in range(chunks):
        rounded = jnp.einsum(
            "slc,cn->sln", gated[:, q], out_weight, preferred_element_type=jnp.float32
        ).astype(jnp.bfloat16)
        outs.append(lax.psum_scatter(rounded, "chan", scatter_dimension=0, tiled=False))
    return jnp.concatenate(outs, 0)


def solution(mesh):
    return jax.shard_map(
        local,
        mesh=mesh,
        in_specs=(
            P(("ctx", "chan"), None),
            P(None, None, "chan"),
            P(None, None, "chan"),
            P(None, "chan"),
            P(None, "chan"),
            P("chan"),
            P("chan", None),
        ),
        out_specs=P(("ctx", "chan"), None),
        check_vma=False,
    )
```

```python
import functools

import jax
import jax.numpy as jnp
from jax import lax
from jax.experimental import pallas as pl
from jax.experimental.pallas import tpu as pltpu
from jax.sharding import PartitionSpec as P

SEGS = 8
LANES = 128
CHUNKS = 1


def from_behind(array, axis, by):
    size = lax.axis_size(axis)
    pairs = [(i, i + by) for i in range(size) if 0 <= i + by < size]
    return lax.ppermute(array, axis, pairs)


def scan_kernel(x_ref, p_ref, g_ref, *refs, steps, segs, with_y):
    if with_y:
        refs, staged = refs[:-1], refs[-1]
    modes = p_ref.shape[0]
    lanes = x_ref.shape[1]
    poles = [jnp.broadcast_to(p_ref[pl.ds(r, 1), :], (segs, lanes)) for r in range(modes)]
    if with_y:
        q_ref, skip_ref, s0_ref, y_ref, end_ref = refs
        skip = jnp.broadcast_to(skip_ref[...], (segs, lanes))
        gains = [jnp.broadcast_to(g_ref[pl.ds(r, 1), :], (segs, lanes)) for r in range(modes)]
        start = tuple(s0_ref[r] for r in range(modes))
    else:
        tw_ref, end_ref, own_ref = refs
        start = tuple(jnp.zeros((segs, lanes), jnp.float32) for r in range(modes))

    def body(k, state):
        drive = x_ref[pl.ds(k, segs, stride=steps), :]
        state = tuple(poles[r] * state[r] + drive for r in range(modes))
        if with_y:
            acc = gains[0] * state[0]
            for r in range(1, modes):
                acc = acc + gains[r] * state[r]
            rows = pl.ds(k, segs, stride=steps)
            staged[rows, :] = q_ref[rows, :] * (acc + skip * drive)
        return state

    state = lax.fori_loop(0, steps, body, start, unroll=8)
    for r in range(modes):
        end_ref[r] = state[r]
    if not with_y:
        for r in range(modes):
            own = jnp.sum(tw_ref[r] * state[r], axis=0, keepdims=True)
            for b in range(own_ref.shape[0]):
                own_ref[b, pl.ds(r, 1), :] = own
    if with_y:
        y_ref[...] = staged[...].astype(y_ref.dtype)


def modal_scan(x, poles, gains, init, with_y, query=None, skip=None, blocks=1):
    seq_rows, chans = x.shape
    modes = poles.shape[0]
    steps = seq_rows // SEGS
    state_spec = pl.BlockSpec((modes, SEGS, LANES), lambda i: (0, 0, i))
    param_spec = pl.BlockSpec((modes, LANES), lambda i: (0, i))
    x_spec = pl.BlockSpec((seq_rows, LANES), lambda i: (0, i))
    end_shape = jax.ShapeDtypeStruct((modes, SEGS, chans), jnp.float32)
    in_specs = [x_spec, param_spec, param_spec]
    operands = [x, poles, gains]
    if with_y:
        out_shape = (jax.ShapeDtypeStruct((seq_rows, chans), jnp.bfloat16), end_shape)
        out_specs = (x_spec, state_spec)
        in_specs += [x_spec, pl.BlockSpec((1, LANES), lambda i: (0, i)), state_spec]
        operands += [query, skip.reshape(1, chans), init]
    else:
        out_shape = (end_shape, jax.ShapeDtypeStruct((blocks, modes, chans), jnp.float32))
        out_specs = (state_spec, pl.BlockSpec((blocks, modes, LANES), lambda i: (0, 0, i)))
        in_specs.append(state_spec)
        operands.append(init)
    scratch = [pltpu.VMEM((seq_rows, LANES), jnp.float32)] if with_y else []
    return pl.pallas_call(
        functools.partial(scan_kernel, steps=steps, segs=SEGS, with_y=with_y),
        grid=(chans // LANES,),
        scratch_shapes=scratch,
        in_specs=in_specs,
        out_specs=out_specs,
        out_shape=out_shape,
    )(*operands)


def local(tokens, in_weight, short_weight, decay_rate, residue, skip_gain, out_weight):
    group_chans = in_weight.shape[2]
    filter_taps = short_weight.shape[0]
    modes = decay_rate.shape[0]
    width = lax.axis_size("chan")
    tail = tokens[tokens.shape[0] - (filter_taps - 1) :]
    earlier_tokens = jnp.zeros_like(tail)
    for target in range(width):
        pairs = [
            ((block - 1) * width + width - 1, block * width + target)
            for block in range(1, lax.axis_size("ctx"))
        ]
        earlier_tokens = earlier_tokens + lax.ppermute(tail, ("ctx", "chan"), pairs)
    chunks = CHUNKS
    rows = tokens.shape[0] // chunks
    parts = []
    for q in range(chunks):
        gathered = lax.all_gather(tokens[q * rows : (q + 1) * rows], "chan", axis=0)
        parts.append(
            jnp.einsum("sld,jdc->sljc", gathered, in_weight, preferred_element_type=jnp.float32).astype(
                jnp.bfloat16
            )
        )
    sources = parts[0].shape[0]
    seq_rows = sources * chunks * rows
    projected = jnp.stack(parts, 1).reshape(seq_rows, 3, group_chans)
    earlier_rows = jnp.einsum(
        "ld,jdc->ljc", earlier_tokens, in_weight, preferred_element_type=jnp.float32
    ).astype(jnp.bfloat16)
    padded = jnp.concatenate([earlier_rows, projected], 0)

    def feature(kind):
        total = short_weight[0, kind] * padded[filter_taps - 1 :, kind].astype(jnp.float32)
        for offset in range(1, filter_taps):
            total = total + short_weight[offset, kind] * padded[
                filter_taps - 1 - offset : filter_taps - 1 - offset + seq_rows, kind
            ].astype(jnp.float32)
        return total

    query_part = feature(0)
    driven = feature(1) * feature(2)

    seg_len = seq_rows // SEGS
    poles = jnp.exp(-decay_rate)
    mode_gain = residue * jnp.sqrt(2.0 * decay_rate)
    seg_pos = jnp.arange(SEGS, dtype=jnp.float32)
    tail_weight = jnp.exp(-decay_rate[:, None, :] * seg_len * (SEGS - 1.0 - seg_pos)[None, :, None])
    blocks = lax.axis_size("ctx")
    mine = lax.axis_index("ctx")
    seg_end, own_copies = modal_scan(driven, poles, mode_gain, tail_weight, False, blocks=blocks)
    states = lax.all_to_all(own_copies, "ctx", 0, 0)
    back = (mine - 1 - jnp.arange(blocks)).astype(jnp.float32)
    block_weight = jnp.where(
        (back >= 0.0)[:, None, None],
        jnp.exp(-decay_rate[None] * seq_rows * jnp.maximum(back, 0.0)[:, None, None]),
        0.0,
    )
    entering = jnp.sum(block_weight * states, 0)
    seg_gap = seg_pos[:, None] - 1.0 - seg_pos[None, :]
    seg_mix = jnp.where(
        (seg_gap >= 0.0)[:, :, None, None],
        jnp.exp(-decay_rate[None, None] * seg_len * jnp.maximum(seg_gap, 0.0)[:, :, None, None]),
        0.0,
    )
    seg_init = jnp.einsum("jirc,ric->rjc", seg_mix, seg_end, precision=lax.Precision.HIGHEST)
    seg_init = seg_init + jnp.exp(
        -decay_rate[:, None, :] * seg_len * seg_pos[None, :, None]
    ) * entering[:, None, :]
    gated, _ = modal_scan(driven, poles, mode_gain, seg_init, True, query_part, skip_gain)
    gated = gated.reshape(sources, chunks, rows, group_chans)
    outs = []
    for q in range(chunks):
        rounded = jnp.einsum(
            "slc,cn->sln", gated[:, q], out_weight, preferred_element_type=jnp.float32
        ).astype(jnp.bfloat16)
        outs.append(lax.psum_scatter(rounded, "chan", scatter_dimension=0, tiled=False))
    return jnp.concatenate(outs, 0)


def solution(mesh):
    return jax.shard_map(
        local,
        mesh=mesh,
        in_specs=(
            P(("ctx", "chan"), None),
            P(None, None, "chan"),
            P(None, None, "chan"),
            P(None, "chan"),
            P(None, "chan"),
            P("chan"),
            P("chan", None),
        ),
        out_specs=P(("ctx", "chan"), None),
        check_vma=False,
    )
```

```python
import functools

import jax
import jax.numpy as jnp
from jax import lax
from jax.experimental import pallas as pl
from jax.experimental.pallas import tpu as pltpu
from jax.sharding import PartitionSpec as P

SEGS = 8
LANES = 128
CHUNKS = 1


def from_behind(array, axis, by):
    size = lax.axis_size(axis)
    pairs = [(i, i + by) for i in range(size) if 0 <= i + by < size]
    return lax.ppermute(array, axis, pairs)


def scan_kernel(x_ref, p_ref, g_ref, *refs, steps, segs, with_y):
    if with_y:
        refs, staged = refs[:-1], refs[-1]
    modes = p_ref.shape[0]
    lanes = x_ref.shape[1]
    poles = [jnp.broadcast_to(p_ref[pl.ds(r, 1), :], (segs, lanes)) for r in range(modes)]
    if with_y:
        q_ref, skip_ref, s0_ref, y_ref, end_ref = refs
        skip = jnp.broadcast_to(skip_ref[...], (segs, lanes))
        gains = [jnp.broadcast_to(g_ref[pl.ds(r, 1), :], (segs, lanes)) for r in range(modes)]
        start = tuple(s0_ref[r] for r in range(modes))
    else:
        tw_ref, end_ref, own_ref = refs
        start = tuple(jnp.zeros((segs, lanes), jnp.float32) for r in range(modes))

    def body(k, state):
        drive = x_ref[pl.ds(k, segs, stride=steps), :]
        state = tuple(poles[r] * state[r] + drive for r in range(modes))
        if with_y:
            terms = [gains[r] * state[r] for r in range(modes)]
            while len(terms) > 1:
                terms = [terms[i] + terms[i + 1] for i in range(0, len(terms) - 1, 2)] + terms[len(terms) - len(terms) % 2 :]
            acc = terms[0]
            rows = pl.ds(k, segs, stride=steps)
            staged[rows, :] = q_ref[rows, :] * (acc + skip * drive)
        return state

    state = lax.fori_loop(0, steps, body, start, unroll=8)
    for r in range(modes):
        end_ref[r] = state[r]
    if not with_y:
        for r in range(modes):
            own = jnp.sum(tw_ref[r] * state[r], axis=0, keepdims=True)
            for b in range(own_ref.shape[0]):
                own_ref[b, pl.ds(r, 1), :] = own
    if with_y:
        y_ref[...] = staged[...].astype(y_ref.dtype)


def modal_scan(x, poles, gains, init, with_y, query=None, skip=None, blocks=1):
    seq_rows, chans = x.shape
    modes = poles.shape[0]
    steps = seq_rows // SEGS
    state_spec = pl.BlockSpec((modes, SEGS, LANES), lambda i: (0, 0, i))
    param_spec = pl.BlockSpec((modes, LANES), lambda i: (0, i))
    x_spec = pl.BlockSpec((seq_rows, LANES), lambda i: (0, i))
    end_shape = jax.ShapeDtypeStruct((modes, SEGS, chans), jnp.float32)
    in_specs = [x_spec, param_spec, param_spec]
    operands = [x, poles, gains]
    if with_y:
        out_shape = (jax.ShapeDtypeStruct((seq_rows, chans), jnp.bfloat16), end_shape)
        out_specs = (x_spec, state_spec)
        in_specs += [x_spec, pl.BlockSpec((1, LANES), lambda i: (0, i)), state_spec]
        operands += [query, skip.reshape(1, chans), init]
    else:
        out_shape = (end_shape, jax.ShapeDtypeStruct((blocks, modes, chans), jnp.float32))
        out_specs = (state_spec, pl.BlockSpec((blocks, modes, LANES), lambda i: (0, 0, i)))
        in_specs.append(state_spec)
        operands.append(init)
    scratch = [pltpu.VMEM((seq_rows, LANES), jnp.float32)] if with_y else []
    return pl.pallas_call(
        functools.partial(scan_kernel, steps=steps, segs=SEGS, with_y=with_y),
        grid=(chans // LANES,),
        scratch_shapes=scratch,
        in_specs=in_specs,
        out_specs=out_specs,
        out_shape=out_shape,
    )(*operands)


def local(tokens, in_weight, short_weight, decay_rate, residue, skip_gain, out_weight):
    group_chans = in_weight.shape[2]
    filter_taps = short_weight.shape[0]
    modes = decay_rate.shape[0]
    width = lax.axis_size("chan")
    tail = tokens[tokens.shape[0] - (filter_taps - 1) :]
    earlier_tokens = jnp.zeros_like(tail)
    for target in range(width):
        pairs = [
            ((block - 1) * width + width - 1, block * width + target)
            for block in range(1, lax.axis_size("ctx"))
        ]
        earlier_tokens = earlier_tokens + lax.ppermute(tail, ("ctx", "chan"), pairs)
    chunks = CHUNKS
    rows = tokens.shape[0] // chunks
    parts = []
    for q in range(chunks):
        gathered = lax.all_gather(tokens[q * rows : (q + 1) * rows], "chan", axis=0)
        parts.append(
            jnp.einsum("sld,jdc->sljc", gathered, in_weight, preferred_element_type=jnp.float32).astype(
                jnp.bfloat16
            )
        )
    sources = parts[0].shape[0]
    seq_rows = sources * chunks * rows
    projected = jnp.stack(parts, 1).reshape(seq_rows, 3, group_chans)
    earlier_rows = jnp.einsum(
        "ld,jdc->ljc", earlier_tokens, in_weight, preferred_element_type=jnp.float32
    ).astype(jnp.bfloat16)
    padded = jnp.concatenate([earlier_rows, projected], 0)

    def feature(kind):
        total = short_weight[0, kind] * padded[filter_taps - 1 :, kind].astype(jnp.float32)
        for offset in range(1, filter_taps):
            total = total + short_weight[offset, kind] * padded[
                filter_taps - 1 - offset : filter_taps - 1 - offset + seq_rows, kind
            ].astype(jnp.float32)
        return total

    query_part = feature(0)
    driven = feature(1) * feature(2)

    seg_len = seq_rows // SEGS
    poles = jnp.exp(-decay_rate)
    mode_gain = residue * jnp.sqrt(2.0 * decay_rate)
    seg_pos = jnp.arange(SEGS, dtype=jnp.float32)
    tail_weight = jnp.exp(-decay_rate[:, None, :] * seg_len * (SEGS - 1.0 - seg_pos)[None, :, None])
    blocks = lax.axis_size("ctx")
    mine = lax.axis_index("ctx")
    seg_end, own_copies = modal_scan(driven, poles, mode_gain, tail_weight, False, blocks=blocks)
    states = lax.all_to_all(own_copies, "ctx", 0, 0)
    back = (mine - 1 - jnp.arange(blocks)).astype(jnp.float32)
    block_weight = jnp.where(
        (back >= 0.0)[:, None, None],
        jnp.exp(-decay_rate[None] * seq_rows * jnp.maximum(back, 0.0)[:, None, None]),
        0.0,
    )
    entering = jnp.sum(block_weight * states, 0)
    seg_gap = seg_pos[:, None] - 1.0 - seg_pos[None, :]
    seg_mix = jnp.where(
        (seg_gap >= 0.0)[:, :, None, None],
        jnp.exp(-decay_rate[None, None] * seg_len * jnp.maximum(seg_gap, 0.0)[:, :, None, None]),
        0.0,
    )
    seg_init = jnp.einsum("jirc,ric->rjc", seg_mix, seg_end, precision=lax.Precision.HIGHEST)
    seg_init = seg_init + jnp.exp(
        -decay_rate[:, None, :] * seg_len * seg_pos[None, :, None]
    ) * entering[:, None, :]
    gated, _ = modal_scan(driven, poles, mode_gain, seg_init, True, query_part, skip_gain)
    gated = gated.reshape(sources, chunks, rows, group_chans)
    outs = []
    for q in range(chunks):
        rounded = jnp.einsum(
            "slc,cn->sln", gated[:, q], out_weight, preferred_element_type=jnp.float32
        ).astype(jnp.bfloat16)
        outs.append(lax.psum_scatter(rounded, "chan", scatter_dimension=0, tiled=False))
    return jnp.concatenate(outs, 0)


def solution(mesh):
    return jax.shard_map(
        local,
        mesh=mesh,
        in_specs=(
            P(("ctx", "chan"), None),
            P(None, None, "chan"),
            P(None, None, "chan"),
            P(None, "chan"),
            P(None, "chan"),
            P("chan"),
            P("chan", None),
        ),
        out_specs=P(("ctx", "chan"), None),
        check_vma=False,
    )
```

```python
import functools

import jax
import jax.numpy as jnp
from jax import lax
from jax.experimental import pallas as pl
from jax.experimental.pallas import tpu as pltpu
from jax.sharding import PartitionSpec as P

SEGS = 8
LANES = 128
CHUNKS = 1


def from_behind(array, axis, by):
    size = lax.axis_size(axis)
    pairs = [(i, i + by) for i in range(size) if 0 <= i + by < size]
    return lax.ppermute(array, axis, pairs)


def scan_kernel(x_ref, p_ref, g_ref, *refs, steps, segs, with_y):
    if with_y:
        refs, staged = refs[:-1], refs[-1]
    modes = p_ref.shape[0]
    lanes = x_ref.shape[1]
    poles = [jnp.broadcast_to(p_ref[pl.ds(r, 1), :], (segs, lanes)) for r in range(modes)]
    if with_y:
        q_ref, skip_ref, s0_ref, y_ref, end_ref = refs
        skip = jnp.broadcast_to(skip_ref[...], (segs, lanes))
        gains = [jnp.broadcast_to(g_ref[pl.ds(r, 1), :], (segs, lanes)) for r in range(modes)]
        start = tuple(s0_ref[r] for r in range(modes))
    else:
        tw_ref, end_ref, own_ref = refs
        start = tuple(jnp.zeros((segs, lanes), jnp.float32) for r in range(modes))

    def body(k, state):
        drive = x_ref[pl.ds(k, segs, stride=steps), :]
        state = tuple(poles[r] * state[r] + drive for r in range(modes))
        if with_y:
            terms = [gains[r] * state[r] for r in range(modes)]
            while len(terms) > 1:
                terms = [terms[i] + terms[i + 1] for i in range(0, len(terms) - 1, 2)] + terms[len(terms) - len(terms) % 2 :]
            acc = terms[0]
            rows = pl.ds(k, segs, stride=steps)
            staged[rows, :] = q_ref[rows, :] * (acc + skip * drive)
        return state

    state = lax.fori_loop(0, steps, body, start, unroll=16)
    for r in range(modes):
        end_ref[r] = state[r]
    if not with_y:
        for r in range(modes):
            own = jnp.sum(tw_ref[r] * state[r], axis=0, keepdims=True)
            for b in range(own_ref.shape[0]):
                own_ref[b, pl.ds(r, 1), :] = own
    if with_y:
        y_ref[...] = staged[...].astype(y_ref.dtype)


def modal_scan(x, poles, gains, init, with_y, query=None, skip=None, blocks=1):
    seq_rows, chans = x.shape
    modes = poles.shape[0]
    steps = seq_rows // SEGS
    state_spec = pl.BlockSpec((modes, SEGS, LANES), lambda i: (0, 0, i))
    param_spec = pl.BlockSpec((modes, LANES), lambda i: (0, i))
    x_spec = pl.BlockSpec((seq_rows, LANES), lambda i: (0, i))
    end_shape = jax.ShapeDtypeStruct((modes, SEGS, chans), jnp.float32)
    in_specs = [x_spec, param_spec, param_spec]
    operands = [x, poles, gains]
    if with_y:
        out_shape = (jax.ShapeDtypeStruct((seq_rows, chans), jnp.bfloat16), end_shape)
        out_specs = (x_spec, state_spec)
        in_specs += [x_spec, pl.BlockSpec((1, LANES), lambda i: (0, i)), state_spec]
        operands += [query, skip.reshape(1, chans), init]
    else:
        out_shape = (end_shape, jax.ShapeDtypeStruct((blocks, modes, chans), jnp.float32))
        out_specs = (state_spec, pl.BlockSpec((blocks, modes, LANES), lambda i: (0, 0, i)))
        in_specs.append(state_spec)
        operands.append(init)
    scratch = [pltpu.VMEM((seq_rows, LANES), jnp.float32)] if with_y else []
    return pl.pallas_call(
        functools.partial(scan_kernel, steps=steps, segs=SEGS, with_y=with_y),
        grid=(chans // LANES,),
        scratch_shapes=scratch,
        in_specs=in_specs,
        out_specs=out_specs,
        out_shape=out_shape,
    )(*operands)


def local(tokens, in_weight, short_weight, decay_rate, residue, skip_gain, out_weight):
    group_chans = in_weight.shape[2]
    filter_taps = short_weight.shape[0]
    modes = decay_rate.shape[0]
    width = lax.axis_size("chan")
    tail = tokens[tokens.shape[0] - (filter_taps - 1) :]
    earlier_tokens = jnp.zeros_like(tail)
    for target in range(width):
        pairs = [
            ((block - 1) * width + width - 1, block * width + target)
            for block in range(1, lax.axis_size("ctx"))
        ]
        earlier_tokens = earlier_tokens + lax.ppermute(tail, ("ctx", "chan"), pairs)
    chunks = CHUNKS
    rows = tokens.shape[0] // chunks
    parts = []
    for q in range(chunks):
        gathered = lax.all_gather(tokens[q * rows : (q + 1) * rows], "chan", axis=0)
        parts.append(
            jnp.einsum("sld,jdc->sljc", gathered, in_weight, preferred_element_type=jnp.float32).astype(
                jnp.bfloat16
            )
        )
    sources = parts[0].shape[0]
    seq_rows = sources * chunks * rows
    projected = jnp.stack(parts, 1).reshape(seq_rows, 3, group_chans)
    earlier_rows = jnp.einsum(
        "ld,jdc->ljc", earlier_tokens, in_weight, preferred_element_type=jnp.float32
    ).astype(jnp.bfloat16)
    padded = jnp.concatenate([earlier_rows, projected], 0)

    def feature(kind):
        total = short_weight[0, kind] * padded[filter_taps - 1 :, kind].astype(jnp.float32)
        for offset in range(1, filter_taps):
            total = total + short_weight[offset, kind] * padded[
                filter_taps - 1 - offset : filter_taps - 1 - offset + seq_rows, kind
            ].astype(jnp.float32)
        return total

    query_part = feature(0)
    driven = feature(1) * feature(2)

    seg_len = seq_rows // SEGS
    poles = jnp.exp(-decay_rate)
    mode_gain = residue * jnp.sqrt(2.0 * decay_rate)
    seg_pos = jnp.arange(SEGS, dtype=jnp.float32)
    tail_weight = jnp.exp(-decay_rate[:, None, :] * seg_len * (SEGS - 1.0 - seg_pos)[None, :, None])
    blocks = lax.axis_size("ctx")
    mine = lax.axis_index("ctx")
    seg_end, own_copies = modal_scan(driven, poles, mode_gain, tail_weight, False, blocks=blocks)
    states = lax.all_to_all(own_copies, "ctx", 0, 0)
    back = (mine - 1 - jnp.arange(blocks)).astype(jnp.float32)
    block_weight = jnp.where(
        (back >= 0.0)[:, None, None],
        jnp.exp(-decay_rate[None] * seq_rows * jnp.maximum(back, 0.0)[:, None, None]),
        0.0,
    )
    entering = jnp.sum(block_weight * states, 0)
    seg_gap = seg_pos[:, None] - 1.0 - seg_pos[None, :]
    seg_mix = jnp.where(
        (seg_gap >= 0.0)[:, :, None, None],
        jnp.exp(-decay_rate[None, None] * seg_len * jnp.maximum(seg_gap, 0.0)[:, :, None, None]),
        0.0,
    )
    seg_init = jnp.einsum("jirc,ric->rjc", seg_mix, seg_end, precision=lax.Precision.HIGHEST)
    seg_init = seg_init + jnp.exp(
        -decay_rate[:, None, :] * seg_len * seg_pos[None, :, None]
    ) * entering[:, None, :]
    gated, _ = modal_scan(driven, poles, mode_gain, seg_init, True, query_part, skip_gain)
    gated = gated.reshape(sources, chunks, rows, group_chans)
    outs = []
    for q in range(chunks):
        rounded = jnp.einsum(
            "slc,cn->sln", gated[:, q], out_weight, preferred_element_type=jnp.float32
        ).astype(jnp.bfloat16)
        outs.append(lax.psum_scatter(rounded, "chan", scatter_dimension=0, tiled=False))
    return jnp.concatenate(outs, 0)


def solution(mesh):
    return jax.shard_map(
        local,
        mesh=mesh,
        in_specs=(
            P(("ctx", "chan"), None),
            P(None, None, "chan"),
            P(None, None, "chan"),
            P(None, "chan"),
            P(None, "chan"),
            P("chan"),
            P("chan", None),
        ),
        out_specs=P(("ctx", "chan"), None),
        check_vma=False,
    )
```

```python
import functools

import jax
import jax.numpy as jnp
from jax import lax
from jax.experimental import pallas as pl
from jax.experimental.pallas import tpu as pltpu
from jax.sharding import PartitionSpec as P

SEGS = 8
LANES = 128
CHUNKS = 1


def from_behind(array, axis, by):
    size = lax.axis_size(axis)
    pairs = [(i, i + by) for i in range(size) if 0 <= i + by < size]
    return lax.ppermute(array, axis, pairs)


def scan_kernel(x_ref, p_ref, g_ref, *refs, steps, segs, with_y):
    if with_y:
        refs, staged = refs[:-1], refs[-1]
    modes = p_ref.shape[0]
    lanes = x_ref.shape[1]
    poles = [jnp.broadcast_to(p_ref[pl.ds(r, 1), :], (segs, lanes)) for r in range(modes)]
    if with_y:
        q_ref, skip_ref, s0_ref, y_ref, end_ref = refs
        skip = jnp.broadcast_to(skip_ref[...], (segs, lanes))
        gains = [jnp.broadcast_to(g_ref[pl.ds(r, 1), :], (segs, lanes)) for r in range(modes)]
        start = tuple(s0_ref[r] for r in range(modes))
    else:
        tw_ref, end_ref, own_ref = refs
        start = tuple(jnp.zeros((segs, lanes), jnp.float32) for r in range(modes))

    def body(k, state):
        drive = x_ref[pl.ds(k, segs, stride=steps), :]
        state = tuple(poles[r] * state[r] + drive for r in range(modes))
        if with_y:
            terms = [gains[r] * state[r] for r in range(modes)]
            while len(terms) > 1:
                terms = [terms[i] + terms[i + 1] for i in range(0, len(terms) - 1, 2)] + terms[len(terms) - len(terms) % 2 :]
            acc = terms[0]
            rows = pl.ds(k, segs, stride=steps)
            staged[rows, :] = q_ref[rows, :] * (acc + skip * drive)
        return state

    state = lax.fori_loop(0, steps, body, start, unroll=8)
    for r in range(modes):
        end_ref[r] = state[r]
    if not with_y:
        for r in range(modes):
            own = jnp.sum(tw_ref[r] * state[r], axis=0, keepdims=True)
            for b in range(own_ref.shape[0]):
                own_ref[b, pl.ds(r, 1), :] = own
    if with_y:
        y_ref[...] = staged[...].astype(y_ref.dtype)


def modal_scan(x, poles, gains, init, with_y, query=None, skip=None, blocks=1):
    seq_rows, chans = x.shape
    modes = poles.shape[0]
    steps = seq_rows // SEGS
    state_spec = pl.BlockSpec((modes, SEGS, LANES), lambda i: (0, 0, i))
    param_spec = pl.BlockSpec((modes, LANES), lambda i: (0, i))
    x_spec = pl.BlockSpec((seq_rows, LANES), lambda i: (0, i))
    end_shape = jax.ShapeDtypeStruct((modes, SEGS, chans), jnp.float32)
    in_specs = [x_spec, param_spec, param_spec]
    operands = [x, poles, gains]
    if with_y:
        out_shape = (jax.ShapeDtypeStruct((seq_rows, chans), jnp.bfloat16), end_shape)
        out_specs = (x_spec, state_spec)
        in_specs += [x_spec, pl.BlockSpec((1, LANES), lambda i: (0, i)), state_spec]
        operands += [query, skip.reshape(1, chans), init]
    else:
        out_shape = (end_shape, jax.ShapeDtypeStruct((blocks, modes, chans), jnp.float32))
        out_specs = (state_spec, pl.BlockSpec((blocks, modes, LANES), lambda i: (0, 0, i)))
        in_specs.append(state_spec)
        operands.append(init)
    scratch = [pltpu.VMEM((seq_rows, LANES), jnp.float32)] if with_y else []
    return pl.pallas_call(
        functools.partial(scan_kernel, steps=steps, segs=SEGS, with_y=with_y),
        grid=(chans // LANES,),
        scratch_shapes=scratch,
        in_specs=in_specs,
        out_specs=out_specs,
        out_shape=out_shape,
    )(*operands)


def local(tokens, in_weight, short_weight, decay_rate, residue, skip_gain, out_weight):
    group_chans = in_weight.shape[2]
    filter_taps = short_weight.shape[0]
    modes = decay_rate.shape[0]
    width = lax.axis_size("chan")
    tail = tokens[tokens.shape[0] - (filter_taps - 1) :]
    earlier_tokens = jnp.zeros_like(tail)
    for target in range(width):
        pairs = [
            ((block - 1) * width + width - 1, block * width + target)
            for block in range(1, lax.axis_size("ctx"))
        ]
        earlier_tokens = earlier_tokens + lax.ppermute(tail, ("ctx", "chan"), pairs)
    chunks = CHUNKS
    rows = tokens.shape[0] // chunks
    parts = []
    for q in range(chunks):
        gathered = lax.all_gather(tokens[q * rows : (q + 1) * rows], "chan", axis=0)
        parts.append(
            jnp.einsum("sld,jdc->sljc", gathered, in_weight, preferred_element_type=jnp.float32).astype(
                jnp.bfloat16
            )
        )
    sources = parts[0].shape[0]
    seq_rows = sources * chunks * rows
    projected = jnp.stack(parts, 1).reshape(seq_rows, 3, group_chans)
    earlier_rows = jnp.einsum(
        "ld,jdc->ljc", earlier_tokens, in_weight, preferred_element_type=jnp.float32
    ).astype(jnp.bfloat16)
    padded = jnp.concatenate([earlier_rows, projected], 0)

    def feature(kind):
        total = short_weight[0, kind] * padded[filter_taps - 1 :, kind].astype(jnp.float32)
        for offset in range(1, filter_taps):
            total = total + short_weight[offset, kind] * padded[
                filter_taps - 1 - offset : filter_taps - 1 - offset + seq_rows, kind
            ].astype(jnp.float32)
        return total

    query_part = feature(0)
    driven = feature(1) * feature(2)

    seg_len = seq_rows // SEGS
    poles = jnp.exp(-decay_rate)
    mode_gain = residue * jnp.sqrt(2.0 * decay_rate)
    seg_pos = jnp.arange(SEGS, dtype=jnp.float32)
    tail_weight = jnp.exp(-decay_rate[:, None, :] * seg_len * (SEGS - 1.0 - seg_pos)[None, :, None])
    blocks = lax.axis_size("ctx")
    mine = lax.axis_index("ctx")
    seg_end, own_copies = modal_scan(driven, poles, mode_gain, tail_weight, False, blocks=blocks)
    states = lax.all_to_all(own_copies.astype(jnp.bfloat16), "ctx", 0, 0).astype(jnp.float32)
    back = (mine - 1 - jnp.arange(blocks)).astype(jnp.float32)
    block_weight = jnp.where(
        (back >= 0.0)[:, None, None],
        jnp.exp(-decay_rate[None] * seq_rows * jnp.maximum(back, 0.0)[:, None, None]),
        0.0,
    )
    entering = jnp.sum(block_weight * states, 0)
    seg_gap = seg_pos[:, None] - 1.0 - seg_pos[None, :]
    seg_mix = jnp.where(
        (seg_gap >= 0.0)[:, :, None, None],
        jnp.exp(-decay_rate[None, None] * seg_len * jnp.maximum(seg_gap, 0.0)[:, :, None, None]),
        0.0,
    )
    seg_init = jnp.einsum("jirc,ric->rjc", seg_mix, seg_end, precision=lax.Precision.HIGHEST)
    seg_init = seg_init + jnp.exp(
        -decay_rate[:, None, :] * seg_len * seg_pos[None, :, None]
    ) * entering[:, None, :]
    gated, _ = modal_scan(driven, poles, mode_gain, seg_init, True, query_part, skip_gain)
    gated = gated.reshape(sources, chunks, rows, group_chans)
    outs = []
    for q in range(chunks):
        rounded = jnp.einsum(
            "slc,cn->sln", gated[:, q], out_weight, preferred_element_type=jnp.float32
        ).astype(jnp.bfloat16)
        outs.append(lax.psum_scatter(rounded, "chan", scatter_dimension=0, tiled=False))
    return jnp.concatenate(outs, 0)


def solution(mesh):
    return jax.shard_map(
        local,
        mesh=mesh,
        in_specs=(
            P(("ctx", "chan"), None),
            P(None, None, "chan"),
            P(None, None, "chan"),
            P(None, "chan"),
            P(None, "chan"),
            P("chan"),
            P("chan", None),
        ),
        out_specs=P(("ctx", "chan"), None),
        check_vma=False,
    )
```

```python
import functools

import jax
import jax.numpy as jnp
from jax import lax
from jax.experimental import pallas as pl
from jax.experimental.pallas import tpu as pltpu
from jax.sharding import PartitionSpec as P

SEGS = 8
LANES = 128
CHUNKS = 1


def from_behind(array, axis, by):
    size = lax.axis_size(axis)
    pairs = [(i, i + by) for i in range(size) if 0 <= i + by < size]
    return lax.ppermute(array, axis, pairs)


def scan_kernel(x_ref, p_ref, g_ref, *refs, steps, segs, with_y):
    if with_y:
        refs, staged = refs[:-1], refs[-1]
    modes = p_ref.shape[0]
    lanes = x_ref.shape[1]
    poles = [jnp.broadcast_to(p_ref[pl.ds(r, 1), :], (segs, lanes)) for r in range(modes)]
    if with_y:
        q_ref, skip_ref, s0_ref, y_ref, end_ref = refs
        skip = jnp.broadcast_to(skip_ref[...], (segs, lanes))
        gains = [jnp.broadcast_to(g_ref[pl.ds(r, 1), :], (segs, lanes)) for r in range(modes)]
        start = tuple(s0_ref[r] for r in range(modes))
    else:
        tw_ref, end_ref, own_ref = refs
        start = tuple(jnp.zeros((segs, lanes), jnp.float32) for r in range(modes))

    def body(k, state):
        drive = x_ref[pl.ds(k, segs, stride=steps), :]
        state = tuple(poles[r] * state[r] + drive for r in range(modes))
        if with_y:
            terms = [gains[r] * state[r] for r in range(modes)]
            while len(terms) > 1:
                terms = [terms[i] + terms[i + 1] for i in range(0, len(terms) - 1, 2)] + terms[len(terms) - len(terms) % 2 :]
            acc = terms[0]
            rows = pl.ds(k, segs, stride=steps)
            staged[rows, :] = q_ref[rows, :] * (acc + skip * drive)
        return state

    state = lax.fori_loop(0, steps, body, start, unroll=8)
    for r in range(modes):
        end_ref[r] = state[r]
    if not with_y:
        for r in range(modes):
            own = jnp.sum(tw_ref[r] * state[r], axis=0, keepdims=True)
            for b in range(own_ref.shape[0]):
                own_ref[b, pl.ds(r, 1), :] = own
    if with_y:
        y_ref[...] = staged[...].astype(y_ref.dtype)


def modal_scan(x, poles, gains, init, with_y, query=None, skip=None, blocks=1):
    seq_rows, chans = x.shape
    modes = poles.shape[0]
    steps = seq_rows // SEGS
    state_spec = pl.BlockSpec((modes, SEGS, LANES), lambda i: (0, 0, i))
    param_spec = pl.BlockSpec((modes, LANES), lambda i: (0, i))
    x_spec = pl.BlockSpec((seq_rows, LANES), lambda i: (0, i))
    end_shape = jax.ShapeDtypeStruct((modes, SEGS, chans), jnp.float32)
    in_specs = [x_spec, param_spec, param_spec]
    operands = [x, poles, gains]
    if with_y:
        out_shape = (jax.ShapeDtypeStruct((seq_rows, chans), jnp.bfloat16), end_shape)
        out_specs = (x_spec, state_spec)
        in_specs += [x_spec, pl.BlockSpec((1, LANES), lambda i: (0, i)), state_spec]
        operands += [query, skip.reshape(1, chans), init]
    else:
        out_shape = (end_shape, jax.ShapeDtypeStruct((blocks, modes, chans), jnp.float32))
        out_specs = (state_spec, pl.BlockSpec((blocks, modes, LANES), lambda i: (0, 0, i)))
        in_specs.append(state_spec)
        operands.append(init)
    scratch = [pltpu.VMEM((seq_rows, LANES), jnp.float32)] if with_y else []
    return pl.pallas_call(
        functools.partial(scan_kernel, steps=steps, segs=SEGS, with_y=with_y),
        grid=(chans // LANES,),
        scratch_shapes=scratch,
        in_specs=in_specs,
        out_specs=out_specs,
        out_shape=out_shape,
    )(*operands)


def local(tokens, in_weight, short_weight, decay_rate, residue, skip_gain, out_weight):
    group_chans = in_weight.shape[2]
    filter_taps = short_weight.shape[0]
    modes = decay_rate.shape[0]
    width = lax.axis_size("chan")
    tail = tokens[tokens.shape[0] - (filter_taps - 1) :]
    earlier_tokens = jnp.zeros_like(tail)
    for target in range(width):
        pairs = [
            ((block - 1) * width + width - 1, block * width + target)
            for block in range(1, lax.axis_size("ctx"))
        ]
        earlier_tokens = earlier_tokens + lax.ppermute(tail, ("ctx", "chan"), pairs)
    chunks = CHUNKS
    rows = tokens.shape[0] // chunks
    parts = []
    for q in range(chunks):
        gathered = lax.all_gather(tokens[q * rows : (q + 1) * rows], "chan", axis=0)
        parts.append(
            jnp.einsum("sld,jdc->sljc", gathered, in_weight, preferred_element_type=jnp.float32).astype(
                jnp.bfloat16
            )
        )
    sources = parts[0].shape[0]
    seq_rows = sources * chunks * rows
    projected = jnp.stack(parts, 1).reshape(seq_rows, 3, group_chans)
    earlier_rows = jnp.einsum(
        "ld,jdc->ljc", earlier_tokens, in_weight, preferred_element_type=jnp.float32
    ).astype(jnp.bfloat16)
    padded = jnp.concatenate([earlier_rows, projected], 0)

    def feature(kind):
        total = short_weight[0, kind] * padded[filter_taps - 1 :, kind].astype(jnp.float32)
        for offset in range(1, filter_taps):
            total = total + short_weight[offset, kind] * padded[
                filter_taps - 1 - offset : filter_taps - 1 - offset + seq_rows, kind
            ].astype(jnp.float32)
        return total

    query_part = feature(0)
    driven = feature(1) * feature(2)

    seg_len = seq_rows // SEGS
    poles = jnp.exp(-decay_rate)
    mode_gain = residue * jnp.sqrt(2.0 * decay_rate)
    seg_pos = jnp.arange(SEGS, dtype=jnp.float32)
    tail_weight = jnp.exp(-decay_rate[:, None, :] * seg_len * (SEGS - 1.0 - seg_pos)[None, :, None])
    blocks = lax.axis_size("ctx")
    mine = lax.axis_index("ctx")
    seg_end, own_copies = modal_scan(driven, poles, mode_gain, tail_weight, False, blocks=blocks)
    states = lax.all_to_all(own_copies, "ctx", 0, 0)
    back = (mine - 1 - jnp.arange(blocks)).astype(jnp.float32)
    block_weight = jnp.where(
        (back >= 0.0)[:, None, None],
        jnp.exp(-decay_rate[None] * seq_rows * jnp.maximum(back, 0.0)[:, None, None]),
        0.0,
    )
    entering = jnp.sum(block_weight * states, 0)
    seg_gap = seg_pos[:, None] - 1.0 - seg_pos[None, :]
    seg_mix = jnp.where(
        (seg_gap >= 0.0)[:, :, None, None],
        jnp.exp(-decay_rate[None, None] * seg_len * jnp.maximum(seg_gap, 0.0)[:, :, None, None]),
        0.0,
    )
    seg_init = jnp.einsum("jirc,ric->rjc", seg_mix, seg_end, precision=lax.Precision.HIGHEST)
    seg_init = seg_init + jnp.exp(
        -decay_rate[:, None, :] * seg_len * seg_pos[None, :, None]
    ) * entering[:, None, :]
    gated, _ = modal_scan(driven, poles, mode_gain, seg_init, True, query_part, skip_gain)
    rounded = jnp.dot(gated, out_weight, preferred_element_type=jnp.float32).astype(jnp.bfloat16)
    return lax.psum_scatter(rounded, "chan", scatter_dimension=0, tiled=True)


def solution(mesh):
    return jax.shard_map(
        local,
        mesh=mesh,
        in_specs=(
            P(("ctx", "chan"), None),
            P(None, None, "chan"),
            P(None, None, "chan"),
            P(None, "chan"),
            P(None, "chan"),
            P("chan"),
            P("chan", None),
        ),
        out_specs=P(("ctx", "chan"), None),
        check_vma=False,
    )
```

```python
import functools

import jax
import jax.numpy as jnp
from jax import lax
from jax.experimental import pallas as pl
from jax.experimental.pallas import tpu as pltpu
from jax.sharding import PartitionSpec as P

SEGS = 16
LANES = 128
CHUNKS = 1


def from_behind(array, axis, by):
    size = lax.axis_size(axis)
    pairs = [(i, i + by) for i in range(size) if 0 <= i + by < size]
    return lax.ppermute(array, axis, pairs)


def scan_kernel(x_ref, p_ref, g_ref, *refs, steps, segs, with_y):
    if with_y:
        refs, staged = refs[:-1], refs[-1]
    modes = p_ref.shape[0]
    lanes = x_ref.shape[1]
    halves = segs // 8
    poles = [jnp.broadcast_to(p_ref[pl.ds(r, 1), :], (8, lanes)) for r in range(modes)]
    if with_y:
        q_ref, skip_ref, s0_ref, y_ref, end_ref = refs
        skip = jnp.broadcast_to(skip_ref[...], (8, lanes))
        gains = [jnp.broadcast_to(g_ref[pl.ds(r, 1), :], (8, lanes)) for r in range(modes)]
        start = tuple(s0_ref[r, pl.ds(8 * h, 8), :] for h in range(halves) for r in range(modes))
    else:
        tw_ref, end_ref, own_ref = refs
        start = tuple(jnp.zeros((8, lanes), jnp.float32) for h in range(halves) for r in range(modes))

    def body(k, state):
        new = []
        for h in range(halves):
            rows = pl.ds(k + 8 * h * steps, 8, stride=steps)
            drive = x_ref[rows, :]
            part = [poles[r] * state[h * modes + r] + drive for r in range(modes)]
            new += part
            if with_y:
                terms = [gains[r] * part[r] for r in range(modes)]
                while len(terms) > 1:
                    terms = [terms[i] + terms[i + 1] for i in range(0, len(terms) - 1, 2)] + terms[len(terms) - len(terms) % 2 :]
                staged[rows, :] = q_ref[rows, :] * (terms[0] + skip * drive)
        return tuple(new)

    state = lax.fori_loop(0, steps, body, start, unroll=8)
    for h in range(halves):
        for r in range(modes):
            end_ref[r, pl.ds(8 * h, 8), :] = state[h * modes + r]
    if not with_y:
        for r in range(modes):
            own = sum(
                jnp.sum(tw_ref[r, pl.ds(8 * h, 8), :] * state[h * modes + r], axis=0, keepdims=True)
                for h in range(halves)
            )
            for b in range(own_ref.shape[0]):
                own_ref[b, pl.ds(r, 1), :] = own
    if with_y:
        y_ref[...] = staged[...].astype(y_ref.dtype)


def modal_scan(x, poles, gains, init, with_y, query=None, skip=None, blocks=1):
    seq_rows, chans = x.shape
    modes = poles.shape[0]
    steps = seq_rows // SEGS
    state_spec = pl.BlockSpec((modes, SEGS, LANES), lambda i: (0, 0, i))
    param_spec = pl.BlockSpec((modes, LANES), lambda i: (0, i))
    x_spec = pl.BlockSpec((seq_rows, LANES), lambda i: (0, i))
    end_shape = jax.ShapeDtypeStruct((modes, SEGS, chans), jnp.float32)
    in_specs = [x_spec, param_spec, param_spec]
    operands = [x, poles, gains]
    if with_y:
        out_shape = (jax.ShapeDtypeStruct((seq_rows, chans), jnp.bfloat16), end_shape)
        out_specs = (x_spec, state_spec)
        in_specs += [x_spec, pl.BlockSpec((1, LANES), lambda i: (0, i)), state_spec]
        operands += [query, skip.reshape(1, chans), init]
    else:
        out_shape = (end_shape, jax.ShapeDtypeStruct((blocks, modes, chans), jnp.float32))
        out_specs = (state_spec, pl.BlockSpec((blocks, modes, LANES), lambda i: (0, 0, i)))
        in_specs.append(state_spec)
        operands.append(init)
    scratch = [pltpu.VMEM((seq_rows, LANES), jnp.float32)] if with_y else []
    return pl.pallas_call(
        functools.partial(scan_kernel, steps=steps, segs=SEGS, with_y=with_y),
        grid=(chans // LANES,),
        scratch_shapes=scratch,
        in_specs=in_specs,
        out_specs=out_specs,
        out_shape=out_shape,
    )(*operands)


def local(tokens, in_weight, short_weight, decay_rate, residue, skip_gain, out_weight):
    group_chans = in_weight.shape[2]
    filter_taps = short_weight.shape[0]
    modes = decay_rate.shape[0]
    width = lax.axis_size("chan")
    tail = tokens[tokens.shape[0] - (filter_taps - 1) :]
    earlier_tokens = jnp.zeros_like(tail)
    for target in range(width):
        pairs = [
            ((block - 1) * width + width - 1, block * width + target)
            for block in range(1, lax.axis_size("ctx"))
        ]
        earlier_tokens = earlier_tokens + lax.ppermute(tail, ("ctx", "chan"), pairs)
    chunks = CHUNKS
    rows = tokens.shape[0] // chunks
    parts = []
    for q in range(chunks):
        gathered = lax.all_gather(tokens[q * rows : (q + 1) * rows], "chan", axis=0)
        parts.append(
            jnp.einsum("sld,jdc->sljc", gathered, in_weight, preferred_element_type=jnp.float32).astype(
                jnp.bfloat16
            )
        )
    sources = parts[0].shape[0]
    seq_rows = sources * chunks * rows
    projected = jnp.stack(parts, 1).reshape(seq_rows, 3, group_chans)
    earlier_rows = jnp.einsum(
        "ld,jdc->ljc", earlier_tokens, in_weight, preferred_element_type=jnp.float32
    ).astype(jnp.bfloat16)
    padded = jnp.concatenate([earlier_rows, projected], 0)

    def feature(kind):
        total = short_weight[0, kind] * padded[filter_taps - 1 :, kind].astype(jnp.float32)
        for offset in range(1, filter_taps):
            total = total + short_weight[offset, kind] * padded[
                filter_taps - 1 - offset : filter_taps - 1 - offset + seq_rows, kind
            ].astype(jnp.float32)
        return total

    query_part = feature(0)
    driven = feature(1) * feature(2)

    seg_len = seq_rows // SEGS
    poles = jnp.exp(-decay_rate)
    mode_gain = residue * jnp.sqrt(2.0 * decay_rate)
    seg_pos = jnp.arange(SEGS, dtype=jnp.float32)
    tail_weight = jnp.exp(-decay_rate[:, None, :] * seg_len * (SEGS - 1.0 - seg_pos)[None, :, None])
    blocks = lax.axis_size("ctx")
    mine = lax.axis_index("ctx")
    seg_end, own_copies = modal_scan(driven, poles, mode_gain, tail_weight, False, blocks=blocks)
    states = lax.all_to_all(own_copies, "ctx", 0, 0)
    back = (mine - 1 - jnp.arange(blocks)).astype(jnp.float32)
    block_weight = jnp.where(
        (back >= 0.0)[:, None, None],
        jnp.exp(-decay_rate[None] * seq_rows * jnp.maximum(back, 0.0)[:, None, None]),
        0.0,
    )
    entering = jnp.sum(block_weight * states, 0)
    seg_gap = seg_pos[:, None] - 1.0 - seg_pos[None, :]
    seg_mix = jnp.where(
        (seg_gap >= 0.0)[:, :, None, None],
        jnp.exp(-decay_rate[None, None] * seg_len * jnp.maximum(seg_gap, 0.0)[:, :, None, None]),
        0.0,
    )
    seg_init = jnp.einsum("jirc,ric->rjc", seg_mix, seg_end, precision=lax.Precision.HIGHEST)
    seg_init = seg_init + jnp.exp(
        -decay_rate[:, None, :] * seg_len * seg_pos[None, :, None]
    ) * entering[:, None, :]
    gated, _ = modal_scan(driven, poles, mode_gain, seg_init, True, query_part, skip_gain)
    gated = gated.reshape(sources, chunks, rows, group_chans)
    outs = []
    for q in range(chunks):
        rounded = jnp.einsum(
            "slc,cn->sln", gated[:, q], out_weight, preferred_element_type=jnp.float32
        ).astype(jnp.bfloat16)
        outs.append(lax.psum_scatter(rounded, "chan", scatter_dimension=0, tiled=False))
    return jnp.concatenate(outs, 0)


def solution(mesh):
    return jax.shard_map(
        local,
        mesh=mesh,
        in_specs=(
            P(("ctx", "chan"), None),
            P(None, None, "chan"),
            P(None, None, "chan"),
            P(None, "chan"),
            P(None, "chan"),
            P("chan"),
            P("chan", None),
        ),
        out_specs=P(("ctx", "chan"), None),
        check_vma=False,
    )
```

```python
import functools

import jax
import jax.numpy as jnp
from jax import lax
from jax.experimental import pallas as pl
from jax.experimental.pallas import tpu as pltpu
from jax.sharding import PartitionSpec as P

SEGS = 8
LANES = 128
CHUNKS = 1


def from_behind(array, axis, by):
    size = lax.axis_size(axis)
    pairs = [(i, i + by) for i in range(size) if 0 <= i + by < size]
    return lax.ppermute(array, axis, pairs)


def scan_kernel(x_ref, p_ref, g_ref, *refs, steps, segs, with_y):
    if with_y:
        refs, staged = refs[:-1], refs[-1]
    modes = p_ref.shape[0]
    lanes = x_ref.shape[1]
    poles = [jnp.broadcast_to(p_ref[pl.ds(r, 1), :], (segs, lanes)) for r in range(modes)]
    if with_y:
        q_ref, skip_ref, s0_ref, y_ref, end_ref = refs
        skip = jnp.broadcast_to(skip_ref[...], (segs, lanes))
        gains = [jnp.broadcast_to(g_ref[pl.ds(r, 1), :], (segs, lanes)) for r in range(modes)]
        start = tuple(s0_ref[r] for r in range(modes))
    else:
        tw_ref, end_ref, own_ref = refs
        start = tuple(jnp.zeros((segs, lanes), jnp.float32) for r in range(modes))

    def body(k, state):
        drive = x_ref[pl.ds(k, segs, stride=steps), :]
        state = tuple(poles[r] * state[r] + drive for r in range(modes))
        if with_y:
            terms = [gains[r] * state[r] for r in range(modes)]
            while len(terms) > 1:
                terms = [terms[i] + terms[i + 1] for i in range(0, len(terms) - 1, 2)] + terms[len(terms) - len(terms) % 2 :]
            acc = terms[0]
            rows = pl.ds(k, segs, stride=steps)
            staged[rows, :] = q_ref[rows, :] * (acc + skip * drive)
        return state

    state = lax.fori_loop(0, steps, body, start, unroll=8)
    if with_y:
        for r in range(modes):
            end_ref[r] = state[r]
    else:
        for r in range(modes):
            for i in range(segs):
                end_ref[i, pl.ds(r, 1), :] = state[r][i : i + 1]
        for r in range(modes):
            own = jnp.sum(tw_ref[r] * state[r], axis=0, keepdims=True)
            for b in range(own_ref.shape[0]):
                own_ref[b, pl.ds(r, 1), :] = own
    if with_y:
        y_ref[...] = staged[...].astype(y_ref.dtype)


def modal_scan(x, poles, gains, init, with_y, query=None, skip=None, blocks=1):
    seq_rows, chans = x.shape
    modes = poles.shape[0]
    steps = seq_rows // SEGS
    state_spec = pl.BlockSpec((modes, SEGS, LANES), lambda i: (0, 0, i))
    param_spec = pl.BlockSpec((modes, LANES), lambda i: (0, i))
    x_spec = pl.BlockSpec((seq_rows, LANES), lambda i: (0, i))
    end_shape = jax.ShapeDtypeStruct((modes, SEGS, chans), jnp.float32)
    in_specs = [x_spec, param_spec, param_spec]
    operands = [x, poles, gains]
    if with_y:
        out_shape = (jax.ShapeDtypeStruct((seq_rows, chans), jnp.bfloat16), end_shape)
        out_specs = (x_spec, state_spec)
        in_specs += [x_spec, pl.BlockSpec((1, LANES), lambda i: (0, i)), state_spec]
        operands += [query, skip.reshape(1, chans), init]
    else:
        by_seg = pl.BlockSpec((SEGS, modes, LANES), lambda i: (0, 0, i))
        out_shape = (
            jax.ShapeDtypeStruct((SEGS, modes, chans), jnp.float32),
            jax.ShapeDtypeStruct((blocks, modes, chans), jnp.float32),
        )
        out_specs = (by_seg, pl.BlockSpec((blocks, modes, LANES), lambda i: (0, 0, i)))
        in_specs.append(state_spec)
        operands.append(init)
    scratch = [pltpu.VMEM((seq_rows, LANES), jnp.float32)] if with_y else []
    return pl.pallas_call(
        functools.partial(scan_kernel, steps=steps, segs=SEGS, with_y=with_y),
        grid=(chans // LANES,),
        scratch_shapes=scratch,
        in_specs=in_specs,
        out_specs=out_specs,
        out_shape=out_shape,
    )(*operands)


def local(tokens, in_weight, short_weight, decay_rate, residue, skip_gain, out_weight):
    group_chans = in_weight.shape[2]
    filter_taps = short_weight.shape[0]
    modes = decay_rate.shape[0]
    width = lax.axis_size("chan")
    tail = tokens[tokens.shape[0] - (filter_taps - 1) :]
    earlier_tokens = jnp.zeros_like(tail)
    for target in range(width):
        pairs = [
            ((block - 1) * width + width - 1, block * width + target)
            for block in range(1, lax.axis_size("ctx"))
        ]
        earlier_tokens = earlier_tokens + lax.ppermute(tail, ("ctx", "chan"), pairs)
    chunks = CHUNKS
    rows = tokens.shape[0] // chunks
    parts = []
    for q in range(chunks):
        gathered = lax.all_gather(tokens[q * rows : (q + 1) * rows], "chan", axis=0)
        parts.append(
            jnp.einsum("sld,jdc->sljc", gathered, in_weight, preferred_element_type=jnp.float32).astype(
                jnp.bfloat16
            )
        )
    sources = parts[0].shape[0]
    seq_rows = sources * chunks * rows
    projected = jnp.stack(parts, 1).reshape(seq_rows, 3, group_chans)
    earlier_rows = jnp.einsum(
        "ld,jdc->ljc", earlier_tokens, in_weight, preferred_element_type=jnp.float32
    ).astype(jnp.bfloat16)
    padded = jnp.concatenate([earlier_rows, projected], 0)

    def feature(kind):
        total = short_weight[0, kind] * padded[filter_taps - 1 :, kind].astype(jnp.float32)
        for offset in range(1, filter_taps):
            total = total + short_weight[offset, kind] * padded[
                filter_taps - 1 - offset : filter_taps - 1 - offset + seq_rows, kind
            ].astype(jnp.float32)
        return total

    query_part = feature(0)
    driven = feature(1) * feature(2)

    seg_len = seq_rows // SEGS
    poles = jnp.exp(-decay_rate)
    mode_gain = residue * jnp.sqrt(2.0 * decay_rate)
    seg_pos = jnp.arange(SEGS, dtype=jnp.float32)
    tail_weight = jnp.exp(-decay_rate[:, None, :] * seg_len * (SEGS - 1.0 - seg_pos)[None, :, None])
    blocks = lax.axis_size("ctx")
    mine = lax.axis_index("ctx")
    seg_end, own_copies = modal_scan(driven, poles, mode_gain, tail_weight, False, blocks=blocks)
    states = lax.all_to_all(own_copies, "ctx", 0, 0)
    back = (mine - 1 - jnp.arange(blocks)).astype(jnp.float32)
    block_weight = jnp.where(
        (back >= 0.0)[:, None, None],
        jnp.exp(-decay_rate[None] * seq_rows * jnp.maximum(back, 0.0)[:, None, None]),
        0.0,
    )
    entering = jnp.sum(block_weight * states, 0)
    seg_gap = seg_pos[:, None] - 1.0 - seg_pos[None, :]
    seg_mix = jnp.where(
        (seg_gap >= 0.0)[:, :, None, None],
        jnp.exp(-decay_rate[None, None] * seg_len * jnp.maximum(seg_gap, 0.0)[:, :, None, None]),
        0.0,
    )
    seg_init = jnp.sum(seg_mix * seg_end[None], axis=1).transpose(1, 0, 2)
    seg_init = seg_init + jnp.exp(
        -decay_rate[:, None, :] * seg_len * seg_pos[None, :, None]
    ) * entering[:, None, :]
    gated, _ = modal_scan(driven, poles, mode_gain, seg_init, True, query_part, skip_gain)
    gated = gated.reshape(sources, chunks, rows, group_chans)
    outs = []
    for q in range(chunks):
        rounded = jnp.einsum(
            "slc,cn->sln", gated[:, q], out_weight, preferred_element_type=jnp.float32
        ).astype(jnp.bfloat16)
        outs.append(lax.psum_scatter(rounded, "chan", scatter_dimension=0, tiled=False))
    return jnp.concatenate(outs, 0)


def solution(mesh):
    return jax.shard_map(
        local,
        mesh=mesh,
        in_specs=(
            P(("ctx", "chan"), None),
            P(None, None, "chan"),
            P(None, None, "chan"),
            P(None, "chan"),
            P(None, "chan"),
            P("chan"),
            P("chan", None),
        ),
        out_specs=P(("ctx", "chan"), None),
        check_vma=False,
    )
```
